128 devices in a mesh: rep: 16 (over y, x), ep: 8 (over z, core).
Axes of the slice: x: 4, y: 4, z: 4, core: 2. Of those that a mesh axis runs over, the one named last changes fastest.
Arguments:
- tokens: bfloat16 [16384, 2048], P(('rep', 'ep')), may hold values from -24 to 24
- experts: int32 [16384, 2], P(('rep', 'ep')), may hold values from 0 to 7, all different within a row; in each aligned block of 128 rows (0 to 127, 128 to 255, ...) at most 48 rows name the same one
- gates: bfloat16 [16384, 2], P(('rep', 'ep')), may hold values from 0.099609375 to 1
- w_gate: bfloat16 [8, 2048, 1408], P('ep'), may hold values from -0.125 to 0.125
- w_up: bfloat16 [8, 2048, 1408], P('ep'), may hold values from -0.125 to 0.125
- w_down: bfloat16 [8, 1408, 2048], P('ep'), may hold values from -0.15625 to 0.15625
- cotangent: bfloat16 [16384, 2048], P(('rep', 'ep')), may hold values from -1.1953125 to 1.1953125
Outputs:
- layer_out: bfloat16 [16384, 2048], P(('rep', 'ep'))
- input_grads: bfloat16 [16384, 2048], P(('rep', 'ep'))
- gate_grads: bfloat16 [16384, 2], P(('rep', 'ep'))
- grad_gate: float32 [8, 2048, 1408], P('ep', 'rep')
- grad_up: float32 [8, 2048, 1408], P('ep', 'rep')
- grad_down: float32 [8, 1408, 2048], P('ep', 'rep')
The draws below stay inside these ranges and needn't reach their ends.
Inputs may be any that keep to these rules, and one draw needn't show every extreme that they name: Each row names 2 different experts; the rows of one device name no expert more than 48 times, a bound that some block reaches.
All inputs are finite; a program needn't handle non-finite values.
Results may differ from the reference program's by a relative error of at most 0.013.
Values may be sent and summed in bfloat16 or wider, within the bound.
No kernel may reach another device: no remote copies, remote signals or barrier semaphores. Data moves between devices by JAX's collectives and lax.ppermute only.
A program may use at most 128 MiB of HBM per device.

```python
import math
import jax
import jax.numpy as jnp
import numpy as np
from jax import lax

D = 2048
FF = 1408
TOP = 2
TOK_DEV = 128
EXPERTS = 8
CAP = 48
TOKENS = 16384
N_REP = 16
N_EP = 8


def spiked(result, key, source, target, blocks, factor):
    owner, partner = [(jnp.arange(result.shape[axis_at]) // (result.shape[axis_at] // blocks)).reshape([-1 if axis == axis_at else 1 for axis in range(result.ndim)]) for axis_at in (source, target)]
    chosen = jax.random.permutation(key, blocks)[partner]
    strong = (owner == chosen) | (owner == (partner + blocks // 2) % blocks)
    return jnp.where(strong, factor * result, result)


def block_scale(key, extent, shards, least, top_value):
    loudness = 1.0
    for axis_at, parts in shards:
        heights = jax.random.uniform(jax.random.fold_in(jax.random.fold_in(key, 6), axis_at), (parts,), jnp.float32, least / len(shards), top_value / len(shards))
        loudness = loudness * jnp.repeat(jnp.exp(heights), extent[axis_at] // parts).reshape((-1,) + (1,) * (len(extent) - 1 - axis_at))
    return loudness


def assign_block(stream_key, own, number, rows, number_of, top, reach, lean):
    order = jax.random.permutation(stream_key, number_of)
    crowded, common = shares(number_of, rows * top, reach, lean, True), shares(number_of, rows * top, reach, lean, False)
    places = jnp.arange(number_of)

    def named(tallies, rotation):
        used = int((tallies > 0).sum())
        fixed = max(1, used // 4)
        passed = fixed + (places - fixed + rotation * (used - fixed)) % max(1, number_of - fixed)
        return jnp.zeros((number_of,), jnp.int32).at[order[jnp.where(places < fixed, places, passed)]].set(jnp.asarray(tallies, jnp.int32))

    tallies = jnp.where(number % 4 == 0, named(crowded, number // 4), named(common, number - number // 4 - 1))
    mixed = jax.random.permutation(jax.random.fold_in(own, 3), number_of)
    donor, receiver = mixed[0:number_of // 2 * 2:2], mixed[1:number_of // 2 * 2:2]
    slack = jnp.minimum(tallies[donor] - 1, reach - tallies[receiver]) // 2
    slack = jnp.where((donor == order[0]) | (receiver == order[0]) | (tallies[receiver] == 0), 0, jnp.maximum(slack, 0))
    passed = jax.random.randint(jax.random.fold_in(own, 4), (number_of // 2,), 0, 1 << 20) % (slack + 1)
    tallies = tallies.at[donor].add(-passed).at[receiver].add(passed)
    items = jnp.searchsorted(jnp.cumsum(tallies), jnp.arange(rows * top), side="right").astype(jnp.int32)
    table = items.reshape(top, rows).T
    table = table[jax.random.permutation(jax.random.fold_in(own, 1), rows)]
    rotation = jax.random.randint(jax.random.fold_in(own, 2), (rows, 1), 0, top)
    return jnp.take_along_axis(table, (jnp.arange(top)[None, :] + rotation) % top, axis=1)


def shares(amount, total, bound, slope, full):
    portions = [(1 << 20) // math.isqrt(grade ** slope) + 1 for grade in range(1, amount + 1)]
    largest = bound if full else min(bound, max(-(-total // amount), total * portions[0] // sum(portions)))
    least = 1 if total - largest >= amount - 1 else 0
    given, rest = [largest] + [least] * (amount - 1), total - largest - least * (amount - 1)
    while rest > 0:
        candidates = [i for i in range(1, amount) if given[i] < largest] or [i for i in range(1, amount) if given[i] < bound]
        pool, budget = sum([portions[i] for i in candidates]), rest
        for i in candidates:
            extra = min(bound - given[i], max(1, budget * portions[i] // pool), rest)
            given[i] = given[i] + extra
            rest = rest - extra
    return np.array(given)


def bell_draw(stream_key, dims, scale, limit, split=(), held_as=jnp.bfloat16):
    values = scale * jax.random.normal(stream_key, dims, jnp.float32)
    if split:
        values = values * block_scale(stream_key, dims, split, -0.22, 0.18)
    return jnp.clip(values, -limit, limit).astype(held_as)


def heavy_noise(stream_key, extent, deviation, reach, shards, heavy, kind=jnp.bfloat16):
    entries = deviation * jax.random.normal(stream_key, extent, jnp.float32)
    if shards:
        entries = entries * block_scale(stream_key, extent, shards, -0.22, 0.18)
    return jnp.clip(spiked(entries, jax.random.fold_in(stream_key, 3), *heavy), -reach, reach).astype(kind)


def setup_inputs(seed: int = 0) -> dict:
    streams_of = jax.random.split(jax.random.key(seed), 8)
    tokens = heavy_noise(streams_of[0], (TOKENS, D), 1.0, 24.0, ((0, 128),), (0, 1, 128, 5.5))
    experts_keys = jax.random.split(jax.random.fold_in(streams_of[1], 1), TOKENS // TOK_DEV)
    experts_turns = jax.random.permutation(jax.random.fold_in(streams_of[1], 3), TOKENS // TOK_DEV)
    experts = jax.vmap(lambda own, number: assign_block(jax.random.fold_in(streams_of[1], 2), own, number, TOK_DEV, EXPERTS, TOP, CAP, 2))(experts_keys, experts_turns).reshape((TOKENS, TOP))
    gates = jnp.clip(jnp.exp(math.log(1.0) - 2.306499 * jax.random.uniform(streams_of[2], (TOKENS, TOP), jnp.float32) ** block_scale(streams_of[2], (TOKENS, TOP), ((0, 128),), -0.2, 0.2)), 0.099609375, 1.0).astype(jnp.bfloat16)
    w_gate = bell_draw(streams_of[3], (EXPERTS, D, FF), D ** -0.5, 0.125, ((0, 8),))
    w_up = bell_draw(streams_of[4], (EXPERTS, D, FF), D ** -0.5, 0.125, ((0, 8),))
    w_down = bell_draw(streams_of[5], (EXPERTS, FF, D), FF ** -0.5, 0.15625, ((0, 8),))
    cotangent = bell_draw(streams_of[6], (TOKENS, D), 0.2, 1.1953125, ((0, 128),))
    return {"tokens": tokens, "experts": experts, "gates": gates, "w_gate": w_gate, "w_up": w_up, "w_down": w_down, "cotangent": cotangent}


def store_bf16(value):
    return lax.optimization_barrier(value.astype(jnp.bfloat16)).astype(jnp.float32)


def reference(tokens, experts, gates, w_gate, w_up, w_down, cotangent):
    pair_count = TOK_DEV * TOP
    blocks = TOKENS // TOK_DEV
    flat_exp = experts.reshape(blocks, pair_count)
    onehot = (flat_exp[:, :, None] == jnp.arange(EXPERTS, dtype=jnp.int32)[None, None, :]).astype(jnp.int32)
    slot_rank = jnp.sum((jnp.cumsum(onehot, axis=1) - onehot) * onehot, axis=2)
    slot_index = (flat_exp * CAP + slot_rank).astype(jnp.int32)
    block_ids = jnp.broadcast_to(jnp.arange(blocks, dtype=jnp.int32)[:, None], (blocks, pair_count))
    global_pair = jnp.broadcast_to(jnp.arange(pair_count, dtype=jnp.int32)[None, :], (blocks, pair_count)) + block_ids * pair_count
    table = jnp.zeros((blocks, EXPERTS * CAP), jnp.int32).at[block_ids, slot_index].set(global_pair)
    filled = jnp.zeros((blocks, EXPERTS * CAP), jnp.float32).at[block_ids, slot_index].set(1.0)
    table = table.reshape(N_REP, N_EP, EXPERTS, CAP)
    filled = filled.reshape(N_REP, N_EP, EXPERTS, CAP)
    gate_flat = gates.reshape(-1).astype(jnp.float32)

    def expert_step(carry, expert_id):
        gate_mat = w_gate[expert_id].astype(jnp.float32)
        up_mat = w_up[expert_id].astype(jnp.float32)
        down_mat = w_down[expert_id].astype(jnp.float32)

        def group_step(inner, replica):
            out_acc, grad_acc, dots_acc, sum_gate, sum_up, sum_down = inner
            pair_ids = table[replica, :, expert_id, :].reshape(-1)
            live_rows = filled[replica, :, expert_id, :].reshape(-1)
            token_ids = pair_ids // TOP
            expert_in = tokens[token_ids].astype(jnp.float32) * live_rows[:, None]
            gate_pre = jnp.dot(expert_in, gate_mat)
            up_pre = jnp.dot(expert_in, up_mat)
            sigmoid_g = jax.nn.sigmoid(gate_pre)
            activated = gate_pre * sigmoid_g
            hidden = store_bf16(activated * up_pre)
            expert_out = store_bf16(jnp.dot(hidden, down_mat))
            weight_rows = gate_flat[pair_ids] * live_rows
            out_acc = out_acc.at[token_ids].add(weight_rows[:, None] * expert_out)
            cot_rows = cotangent[token_ids].astype(jnp.float32) * live_rows[:, None]
            dots_acc = dots_acc.at[pair_ids].add(live_rows * jnp.sum(cot_rows * expert_out, axis=1))
            scaled_grad = store_bf16(weight_rows[:, None] * cot_rows)
            hidden_grad = jnp.dot(scaled_grad, down_mat.T)
            gate_delta = store_bf16(hidden_grad * up_pre * sigmoid_g * (1.0 + gate_pre * (1.0 - sigmoid_g)))
            up_delta = store_bf16(hidden_grad * activated)
            row_grads = store_bf16(jnp.dot(gate_delta, gate_mat.T) + jnp.dot(up_delta, up_mat.T))
            grad_acc = grad_acc.at[token_ids].add(row_grads)
            sum_gate = sum_gate + store_bf16(jnp.dot(expert_in.T, gate_delta))
            sum_up = sum_up + store_bf16(jnp.dot(expert_in.T, up_delta))
            sum_down = sum_down + store_bf16(jnp.dot(hidden.T, scaled_grad))
            return (out_acc, grad_acc, dots_acc, sum_gate, sum_up, sum_down), None

        out_acc, grad_acc, dots_acc = carry
        zero_df = jnp.zeros((D, FF), jnp.float32)
        zero_fd = jnp.zeros((FF, D), jnp.float32)
        inner, unused = lax.scan(group_step, (out_acc, grad_acc, dots_acc, zero_df, zero_df, zero_fd), jnp.arange(N_REP, dtype=jnp.int32))
        return (inner[0], inner[1], inner[2]), (inner[3], inner[4], inner[5])

    start = (jnp.zeros((TOKENS, D), jnp.float32), jnp.zeros((TOKENS, D), jnp.float32), jnp.zeros((TOKENS * TOP,), jnp.float32))
    final, stacked = lax.scan(expert_step, start, jnp.arange(EXPERTS, dtype=jnp.int32))
    layer_out = final[0].astype(jnp.bfloat16)
    input_grads = final[1].astype(jnp.bfloat16)
    gate_grads = final[2].reshape(TOKENS, TOP).astype(jnp.bfloat16)
    return (layer_out, input_grads, gate_grads, stacked[0], stacked[1], stacked[2])
```

```python
import jax
import jax.numpy as jnp
from jax import lax
from jax.sharding import PartitionSpec as P


def body(tokens, experts, gates, w_gate, w_up, w_down, cotangent):
    tok_rows, model_width = tokens.shape
    top_count = experts.shape[1]
    n_experts = lax.axis_size("ep")
    n_rep = lax.axis_size("rep")
    capacity = 3 * tok_rows * top_count // (2 * n_experts)
    pair_count = tok_rows * top_count
    gate_mat, up_mat, down_mat = (w_gate[0], w_up[0], w_down[0])
    ff_width = gate_mat.shape[1]
    slots = n_experts * capacity

    flat_exp = experts.reshape(pair_count)
    onehot = (flat_exp[:, None] == jnp.arange(n_experts, dtype=jnp.int32)[None, :]).astype(
        jnp.int32
    )
    slot_rank = jnp.sum((jnp.cumsum(onehot, axis=0) - onehot) * onehot, axis=1)
    slot_index = flat_exp * capacity + slot_rank
    source = jnp.zeros((slots,), jnp.int32).at[slot_index].set(
        jnp.arange(pair_count, dtype=jnp.int32)
    )
    filled = jnp.zeros((slots,), jnp.bfloat16).at[slot_index].set(1.0)
    token_src = source // top_count
    weights = gates.reshape(pair_count, 1).astype(jnp.float32)
    scaled = (weights * jnp.repeat(cotangent, top_count, axis=0).astype(jnp.float32)).astype(
        jnp.bfloat16
    )

    disp = jnp.concatenate(
        [tokens[token_src] * filled[:, None], scaled[source] * filled[:, None]], axis=1
    ).reshape(n_experts, capacity, 2 * model_width)
    recv = lax.all_to_all(disp, "ep", split_axis=0, concat_axis=0, tiled=True).reshape(
        slots, 2 * model_width
    )
    rows_in = recv[:, :model_width]
    out_grads = recv[:, model_width:]

    contract = (((1,), (1,)), ((), ()))
    rows_first = (((0,), (0,)), ((), ()))
    gate_pre = jnp.dot(rows_in, gate_mat, preferred_element_type=jnp.float32)
    up_pre = jnp.dot(rows_in, up_mat, preferred_element_type=jnp.float32)
    sigmoid_g = jax.nn.sigmoid(gate_pre)
    activated = gate_pre * sigmoid_g
    hidden = (activated * up_pre).astype(jnp.bfloat16)
    hidden_grad = lax.dot_general(out_grads, down_mat, contract, preferred_element_type=jnp.float32)
    gate_delta = (hidden_grad * up_pre * sigmoid_g * (1.0 + gate_pre * (1.0 - sigmoid_g))).astype(
        jnp.bfloat16
    )
    up_delta = (hidden_grad * activated).astype(jnp.bfloat16)

    deltas = jnp.concatenate([gate_delta, up_delta], axis=1)
    term_gu = lax.dot_general(
        rows_in, deltas, rows_first, preferred_element_type=jnp.float32
    ).astype(jnp.bfloat16)
    term_down = lax.dot_general(
        hidden, out_grads, rows_first, preferred_element_type=jnp.float32
    ).astype(jnp.bfloat16)
    gu_rows = model_width // n_rep
    down_rows = ff_width // n_rep
    gu_chunk = gu_rows * 2 * ff_width // model_width
    packed = jnp.concatenate(
        [
            term_gu.reshape(n_rep, gu_chunk, model_width),
            term_down.reshape(n_rep, down_rows, model_width),
        ],
        axis=1,
    ).reshape(n_rep * (gu_chunk + down_rows), model_width)
    reduced = lax.optimization_barrier(
        lax.psum_scatter(packed, "rep", scatter_dimension=0, tiled=True)
    )
    red_gu = reduced[:gu_chunk].reshape(gu_rows, 2 * ff_width).astype(jnp.float32)
    grad_gate = red_gu[:, :ff_width]
    grad_up = red_gu[:, ff_width:]
    grad_down = reduced[gu_chunk:].astype(jnp.float32)

    expert_out = jnp.dot(hidden, down_mat, preferred_element_type=jnp.float32).astype(jnp.bfloat16)
    row_grads = (
        lax.dot_general(gate_delta, gate_mat, contract, preferred_element_type=jnp.float32)
        + lax.dot_general(up_delta, up_mat, contract, preferred_element_type=jnp.float32)
    ).astype(jnp.bfloat16)
    back = jnp.concatenate([expert_out, row_grads], axis=1).reshape(
        n_experts, capacity, 2 * model_width
    )
    returned = lax.all_to_all(back, "ep", split_axis=0, concat_axis=0, tiled=True).reshape(
        slots, 2 * model_width
    )
    pair_back = returned[slot_index]
    pair_out = pair_back[:, :model_width]
    pair_grads = pair_back[:, model_width:]
    layer_out = jnp.sum(
        (weights * pair_out.astype(jnp.float32)).reshape(tok_rows, top_count, model_width), axis=1
    ).astype(jnp.bfloat16)
    gate_grads = jnp.einsum(
        "tkd,td->tk",
        pair_out.reshape(tok_rows, top_count, model_width),
        cotangent,
        preferred_element_type=jnp.float32,
    ).astype(jnp.bfloat16)
    input_grads = jnp.sum(
        pair_grads.astype(jnp.float32).reshape(tok_rows, top_count, model_width), axis=1
    ).astype(jnp.bfloat16)
    return (layer_out, input_grads, gate_grads, grad_gate[None], grad_up[None], grad_down[None])


def solution(mesh):
    in_specs = (
        P(("rep", "ep"), None),
        P(("rep", "ep"), None),
        P(("rep", "ep"), None),
        P("ep", None, None),
        P("ep", None, None),
        P("ep", None, None),
        P(("rep", "ep"), None),
    )
    out_specs = (
        P(("rep", "ep"), None),
        P(("rep", "ep"), None),
        P(("rep", "ep"), None),
        P("ep", "rep", None),
        P("ep", "rep", None),
        P("ep", "rep", None),
    )
    return jax.shard_map(body, mesh=mesh, in_specs=in_specs, out_specs=out_specs, check_vma=False)
```

```python
import jax
import jax.numpy as jnp
from jax import lax
from jax.experimental import pallas as pl
from jax.sharding import PartitionSpec as P


def _pack_kernel(xt_ref, gd_ref, ud_ref, ht_ref, og_ref, o_ref):
    ff = gd_ref.shape[1]
    width = og_ref.shape[1]
    rows = xt_ref.shape[0]
    xt = xt_ref[...]
    o_ref[0, :rows, :ff] = jnp.dot(xt, gd_ref[...], preferred_element_type=jnp.float32).astype(
        o_ref.dtype
    )
    o_ref[0, :rows, ff:] = jnp.dot(xt, ud_ref[...], preferred_element_type=jnp.float32).astype(
        o_ref.dtype
    )
    down = jnp.dot(
        ht_ref[...].astype(jnp.bfloat16), og_ref[...], preferred_element_type=jnp.float32
    )
    o_ref[0, rows:, :width] = down.astype(o_ref.dtype)
    o_ref[0, rows:, width:] = jnp.zeros((down.shape[0], 2 * ff - width), o_ref.dtype)


def packed_weight_grads(rows_t, gate_delta, up_delta, hidden_t, recv, n_rep):
    model_width, slots = rows_t.shape
    ff = gate_delta.shape[1]
    gu_rows = model_width // n_rep
    down_rows = ff // n_rep
    flops = 2 * slots * (model_width * 2 * ff + ff * model_width)
    return pl.pallas_call(
        _pack_kernel,
        grid=(n_rep,),
        in_specs=[
            pl.BlockSpec((gu_rows, slots), lambda r: (r, 0)),
            pl.BlockSpec((slots, ff), lambda r: (0, 0)),
            pl.BlockSpec((slots, ff), lambda r: (0, 0)),
            pl.BlockSpec((down_rows, slots), lambda r: (r, 0)),
            pl.BlockSpec((slots, model_width), lambda r: (0, 1)),
        ],
        out_specs=pl.BlockSpec((1, gu_rows + down_rows, 2 * ff), lambda r: (r, 0, 0)),
        out_shape=jax.ShapeDtypeStruct((n_rep, gu_rows + down_rows, 2 * ff), jnp.bfloat16),
        cost_estimate=pl.CostEstimate(
            flops=flops, transcendentals=0, bytes_accessed=2 * n_rep * (gu_rows + down_rows) * 2 * ff
        ),
    )(rows_t, gate_delta, up_delta, hidden_t, recv)


def body(tokens, experts, gates, w_gate, w_up, w_down, cotangent):
    tok_rows, model_width = tokens.shape
    top_count = experts.shape[1]
    n_experts = lax.axis_size("ep")
    n_rep = lax.axis_size("rep")
    capacity = 3 * tok_rows * top_count // (2 * n_experts)
    pair_count = tok_rows * top_count
    gate_mat, up_mat, down_mat = (w_gate[0], w_up[0], w_down[0])
    ff_width = gate_mat.shape[1]
    slots = n_experts * capacity

    flat_exp = experts.reshape(pair_count)
    onehot = (flat_exp[:, None] == jnp.arange(n_experts, dtype=jnp.int32)[None, :]).astype(
        jnp.int32
    )
    slot_rank = jnp.sum((jnp.cumsum(onehot, axis=0) - onehot) * onehot, axis=1)
    slot_index = flat_exp * capacity + slot_rank
    source = jnp.zeros((slots,), jnp.int32).at[slot_index].set(
        jnp.arange(pair_count, dtype=jnp.int32)
    )
    filled = jnp.zeros((slots,), jnp.bfloat16).at[slot_index].set(1.0)
    token_src = source // top_count
    weights = gates.reshape(pair_count, 1).astype(jnp.float32)
    scaled = (weights * jnp.repeat(cotangent, top_count, axis=0).astype(jnp.float32)).astype(
        jnp.bfloat16
    )

    disp = jnp.concatenate(
        [tokens[token_src] * filled[:, None], scaled[source] * filled[:, None]], axis=1
    ).reshape(n_experts, capacity, 2 * model_width)
    recv = lax.all_to_all(disp, "ep", split_axis=0, concat_axis=0, tiled=True).reshape(
        slots, 2 * model_width
    )
    rows_in = recv[:, :model_width]
    out_grads = recv[:, model_width:]

    contract = (((1,), (1,)), ((), ()))
    rows_first = (((0,), (0,)), ((), ()))
    gate_pre = jnp.dot(rows_in, gate_mat, preferred_element_type=jnp.float32)
    up_pre = jnp.dot(rows_in, up_mat, preferred_element_type=jnp.float32)
    sigmoid_g = jax.nn.sigmoid(gate_pre)
    activated = gate_pre * sigmoid_g
    hidden = (activated * up_pre).astype(jnp.bfloat16)
    hidden_grad = lax.dot_general(out_grads, down_mat, contract, preferred_element_type=jnp.float32)
    gate_delta = (hidden_grad * up_pre * sigmoid_g * (1.0 + gate_pre * (1.0 - sigmoid_g))).astype(
        jnp.bfloat16
    )
    up_delta = (hidden_grad * activated).astype(jnp.bfloat16)

    gu_rows = model_width // n_rep
    packed = packed_weight_grads(
        rows_in.T, gate_delta, up_delta, hidden.astype(jnp.float32).T, recv, n_rep
    )
    reduced = lax.optimization_barrier(
        lax.psum_scatter(packed, "rep", scatter_dimension=0, tiled=True)
    )[0]
    grad_gate = reduced[:gu_rows, :ff_width].astype(jnp.float32)
    grad_up = reduced[:gu_rows, ff_width:].astype(jnp.float32)
    grad_down = reduced[gu_rows:, :model_width].astype(jnp.float32)

    expert_out = jnp.dot(hidden, down_mat, preferred_element_type=jnp.float32).astype(jnp.bfloat16)
    row_grads = (
        lax.dot_general(gate_delta, gate_mat, contract, preferred_element_type=jnp.float32)
        + lax.dot_general(up_delta, up_mat, contract, preferred_element_type=jnp.float32)
    ).astype(jnp.bfloat16)
    back = jnp.concatenate([expert_out, row_grads], axis=1).reshape(
        n_experts, capacity, 2 * model_width
    )
    returned = lax.all_to_all(back, "ep", split_axis=0, concat_axis=0, tiled=True).reshape(
        slots, 2 * model_width
    )
    pair_back = returned[slot_index]
    pair_out = pair_back[:, :model_width]
    pair_grads = pair_back[:, model_width:]
    layer_out = jnp.sum(
        (weights * pair_out.astype(jnp.float32)).reshape(tok_rows, top_count, model_width), axis=1
    ).astype(jnp.bfloat16)
    gate_grads = jnp.einsum(
        "tkd,td->tk",
        pair_out.reshape(tok_rows, top_count, model_width),
        cotangent,
        preferred_element_type=jnp.float32,
    ).astype(jnp.bfloat16)
    input_grads = jnp.sum(
        pair_grads.astype(jnp.float32).reshape(tok_rows, top_count, model_width), axis=1
    ).astype(jnp.bfloat16)
    return (layer_out, input_grads, gate_grads, grad_gate[None], grad_up[None], grad_down[None])


def solution(mesh):
    in_specs = (
        P(("rep", "ep"), None),
        P(("rep", "ep"), None),
        P(("rep", "ep"), None),
        P("ep", None, None),
        P("ep", None, None),
        P("ep", None, None),
        P(("rep", "ep"), None),
    )
    out_specs = (
        P(("rep", "ep"), None),
        P(("rep", "ep"), None),
        P(("rep", "ep"), None),
        P("ep", "rep", None),
        P("ep", "rep", None),
        P("ep", "rep", None),
    )
    return jax.shard_map(body, mesh=mesh, in_specs=in_specs, out_specs=out_specs, check_vma=False)
```

```python
import jax
import jax.numpy as jnp
from jax import lax
from jax.experimental import pallas as pl
from jax.experimental.pallas import tpu as pltpu
from jax.sharding import PartitionSpec as P


def _pack_kernel(x_ref, gd_ref, ud_ref, h_ref, og_ref, o_ref, down_ref):
    ff = gd_ref.shape[1]
    width = og_ref.shape[1]
    rows = x_ref.shape[1]
    down_rows = o_ref.shape[1] - rows
    first = (((0,), (0,)), ((), ()))
    r = pl.program_id(0)

    @pl.when(r == 0)
    def _():
        down_ref[...] = lax.dot_general(
            h_ref[...], og_ref[...], first, preferred_element_type=jnp.float32
        )

    x = x_ref[...]
    o_ref[0, :rows, :ff] = lax.dot_general(
        x, gd_ref[...], first, preferred_element_type=jnp.float32
    ).astype(o_ref.dtype)
    o_ref[0, :rows, ff:] = lax.dot_general(
        x, ud_ref[...], first, preferred_element_type=jnp.float32
    ).astype(o_ref.dtype)
    start = pl.multiple_of(r * down_rows, 8)
    o_ref[0, rows:, :width] = down_ref[pl.ds(start, down_rows), :].astype(o_ref.dtype)
    o_ref[0, rows:, width:] = jnp.zeros((down_rows, 2 * ff - width), o_ref.dtype)


def packed_weight_grads(recv, gate_delta, up_delta, hidden, n_rep):
    slots, ff = gate_delta.shape
    model_width = recv.shape[1] // 2
    gu_rows = model_width // n_rep
    down_rows = ff // n_rep
    flops = 2 * slots * (model_width * 2 * ff + ff * model_width)
    return pl.pallas_call(
        _pack_kernel,
        grid=(n_rep,),
        in_specs=[
            pl.BlockSpec((slots, gu_rows), lambda r: (0, r)),
            pl.BlockSpec((slots, ff), lambda r: (0, 0)),
            pl.BlockSpec((slots, ff), lambda r: (0, 0)),
            pl.BlockSpec((slots, ff), lambda r: (0, 0)),
            pl.BlockSpec((slots, model_width), lambda r: (0, 1)),
        ],
        out_specs=pl.BlockSpec((1, gu_rows + down_rows, 2 * ff), lambda r: (r, 0, 0)),
        out_shape=jax.ShapeDtypeStruct((n_rep, gu_rows + down_rows, 2 * ff), jnp.bfloat16),
        scratch_shapes=[pltpu.VMEM((ff, model_width), jnp.float32)],
        compiler_params=pltpu.CompilerParams(dimension_semantics=("arbitrary",)),
        cost_estimate=pl.CostEstimate(
            flops=flops, transcendentals=0, bytes_accessed=2 * n_rep * (gu_rows + down_rows) * 2 * ff
        ),
    )(recv, gate_delta, up_delta, hidden, recv)


def body(tokens, experts, gates, w_gate, w_up, w_down, cotangent):
    tok_rows, model_width = tokens.shape
    top_count = experts.shape[1]
    n_experts = lax.axis_size("ep")
    n_rep = lax.axis_size("rep")
    capacity = 3 * tok_rows * top_count // (2 * n_experts)
    pair_count = tok_rows * top_count
    gate_mat, up_mat, down_mat = (w_gate[0], w_up[0], w_down[0])
    ff_width = gate_mat.shape[1]
    slots = n_experts * capacity

    flat_exp = experts.reshape(pair_count)
    onehot = (flat_exp[:, None] == jnp.arange(n_experts, dtype=jnp.int32)[None, :]).astype(
        jnp.int32
    )
    slot_rank = jnp.sum((jnp.cumsum(onehot, axis=0) - onehot) * onehot, axis=1)
    slot_index = flat_exp * capacity + slot_rank
    source = jnp.zeros((slots,), jnp.int32).at[slot_index].set(
        jnp.arange(pair_count, dtype=jnp.int32)
    )
    filled = jnp.zeros((slots,), jnp.bfloat16).at[slot_index].set(1.0)
    token_src = source // top_count
    weights = gates.reshape(pair_count, 1).astype(jnp.float32)
    slot_weight = weights[source] * filled[:, None].astype(jnp.float32)
    scaled_rows = (slot_weight * cotangent[token_src].astype(jnp.float32)).astype(jnp.bfloat16)

    disp = jnp.concatenate(
        [tokens[token_src] * filled[:, None], scaled_rows], axis=1
    ).reshape(n_experts, capacity, 2 * model_width)
    recv = lax.all_to_all(disp, "ep", split_axis=0, concat_axis=0, tiled=True).reshape(
        slots, 2 * model_width
    )
    rows_in = recv[:, :model_width]
    out_grads = recv[:, model_width:]

    contract = (((1,), (1,)), ((), ()))
    rows_first = (((0,), (0,)), ((), ()))
    gate_pre = jnp.dot(rows_in, gate_mat, preferred_element_type=jnp.float32)
    up_pre = jnp.dot(rows_in, up_mat, preferred_element_type=jnp.float32)
    sigmoid_g = jax.nn.sigmoid(gate_pre)
    activated = gate_pre * sigmoid_g
    hidden = (activated * up_pre).astype(jnp.bfloat16)
    hidden_grad = lax.dot_general(out_grads, down_mat, contract, preferred_element_type=jnp.float32)
    gate_delta = (hidden_grad * up_pre * sigmoid_g * (1.0 + gate_pre * (1.0 - sigmoid_g))).astype(
        jnp.bfloat16
    )
    up_delta = (hidden_grad * activated).astype(jnp.bfloat16)

    gu_rows = model_width // n_rep
    packed = packed_weight_grads(recv, gate_delta, up_delta, hidden, n_rep)
    reduced = lax.optimization_barrier(
        lax.psum_scatter(packed, "rep", scatter_dimension=0, tiled=True)
    )[0]
    grad_gate = reduced[:gu_rows, :ff_width].astype(jnp.float32)
    grad_up = reduced[:gu_rows, ff_width:].astype(jnp.float32)
    grad_down = reduced[gu_rows:, :model_width].astype(jnp.float32)

    expert_out = jnp.dot(hidden, down_mat, preferred_element_type=jnp.float32).astype(jnp.bfloat16)
    row_grads = (
        lax.dot_general(gate_delta, gate_mat, contract, preferred_element_type=jnp.float32)
        + lax.dot_general(up_delta, up_mat, contract, preferred_element_type=jnp.float32)
    ).astype(jnp.bfloat16)
    back = jnp.concatenate([expert_out, row_grads], axis=1).reshape(
        n_experts, capacity, 2 * model_width
    )
    returned = lax.all_to_all(back, "ep", split_axis=0, concat_axis=0, tiled=True).reshape(
        slots, 2 * model_width
    )
    pair_back = returned[slot_index]
    pair_out = pair_back[:, :model_width]
    pair_grads = pair_back[:, model_width:]
    layer_out = jnp.sum(
        (weights * pair_out.astype(jnp.float32)).reshape(tok_rows, top_count, model_width), axis=1
    ).astype(jnp.bfloat16)
    gate_grads = jnp.einsum(
        "tkd,td->tk",
        pair_out.reshape(tok_rows, top_count, model_width),
        cotangent,
        preferred_element_type=jnp.float32,
    ).astype(jnp.bfloat16)
    input_grads = jnp.sum(
        pair_grads.astype(jnp.float32).reshape(tok_rows, top_count, model_width), axis=1
    ).astype(jnp.bfloat16)
    return (layer_out, input_grads, gate_grads, grad_gate[None], grad_up[None], grad_down[None])


def solution(mesh):
    in_specs = (
        P(("rep", "ep"), None),
        P(("rep", "ep"), None),
        P(("rep", "ep"), None),
        P("ep", None, None),
        P("ep", None, None),
        P("ep", None, None),
        P(("rep", "ep"), None),
    )
    out_specs = (
        P(("rep", "ep"), None),
        P(("rep", "ep"), None),
        P(("rep", "ep"), None),
        P("ep", "rep", None),
        P("ep", "rep", None),
        P("ep", "rep", None),
    )
    return jax.shard_map(body, mesh=mesh, in_specs=in_specs, out_specs=out_specs, check_vma=False)
```

```python
import jax
import jax.numpy as jnp
from jax import lax
from jax.experimental import pallas as pl
from jax.experimental.pallas import tpu as pltpu
from jax.sharding import PartitionSpec as P


TILE_ROWS = 16
LANES = 128


def _pack_kernel(x_ref, gd_ref, ud_ref, h_ref, og_ref, o_ref, down_ref):
    ff = gd_ref.shape[1]
    width = og_ref.shape[1]
    rows = x_ref.shape[1]
    down_rows = down_ref.shape[0] // pl.num_programs(0)
    over = 2 * ff - width
    first = (((0,), (0,)), ((), ()))
    r = pl.program_id(0)

    @pl.when(r == 0)
    def _():
        down_ref[...] = lax.dot_general(
            h_ref[...], og_ref[...], first, preferred_element_type=jnp.float32
        )

    x = x_ref[...]
    g = lax.dot_general(x, gd_ref[...], first, preferred_element_type=jnp.float32)
    u = lax.dot_general(x, ud_ref[...], first, preferred_element_type=jnp.float32)
    o_ref[0, :rows, :ff] = g.astype(o_ref.dtype)
    o_ref[0, :rows, ff:] = u[:, : width - ff].astype(o_ref.dtype)
    col_tiles = over // LANES
    for i in range(rows // TILE_ROWS):
        for j in range(col_tiles):
            q, p = divmod(i * col_tiles + j, width // LANES)
            src = u[i * TILE_ROWS : (i + 1) * TILE_ROWS, width - ff + j * LANES :][:, :LANES]
            o_ref[0, rows + q * TILE_ROWS : rows + (q + 1) * TILE_ROWS, p * LANES : (p + 1) * LANES] = (
                src.astype(o_ref.dtype)
            )
    extra = rows * over // width
    start = pl.multiple_of(r * down_rows, 8)
    o_ref[0, rows + extra :, :] = down_ref[pl.ds(start, down_rows), :].astype(o_ref.dtype)


def packed_weight_grads(recv, gate_delta, up_delta, hidden, n_rep):
    slots, ff = gate_delta.shape
    model_width = recv.shape[1] // 2
    gu_rows = model_width // n_rep
    down_rows = ff // n_rep
    extra = gu_rows * (2 * ff - model_width) // model_width
    chunk = gu_rows + extra + down_rows
    flops = 2 * slots * (model_width * 2 * ff + ff * model_width)
    return pl.pallas_call(
        _pack_kernel,
        grid=(n_rep,),
        in_specs=[
            pl.BlockSpec((slots, gu_rows), lambda r: (0, r)),
            pl.BlockSpec((slots, ff), lambda r: (0, 0)),
            pl.BlockSpec((slots, ff), lambda r: (0, 0)),
            pl.BlockSpec((slots, ff), lambda r: (0, 0)),
            pl.BlockSpec((slots, model_width), lambda r: (0, 1)),
        ],
        out_specs=pl.BlockSpec((1, chunk, model_width), lambda r: (r, 0, 0)),
        out_shape=jax.ShapeDtypeStruct((n_rep, chunk, model_width), jnp.bfloat16),
        scratch_shapes=[pltpu.VMEM((ff, model_width), jnp.float32)],
        compiler_params=pltpu.CompilerParams(dimension_semantics=("arbitrary",)),
        cost_estimate=pl.CostEstimate(
            flops=flops, transcendentals=0, bytes_accessed=2 * n_rep * chunk * model_width
        ),
    )(recv, gate_delta, up_delta, hidden, recv)


def unpack_weight_grads(red, gu_rows, ff):
    width = red.shape[1]
    over = 2 * ff - width
    extra = gu_rows * over // width
    gate = red[:gu_rows, :ff]
    up_head = red[:gu_rows, ff:]
    tiles = red[gu_rows : gu_rows + extra].reshape(
        extra // TILE_ROWS, TILE_ROWS, width // LANES, LANES
    )
    tiles = tiles.transpose(0, 2, 1, 3).reshape(
        gu_rows // TILE_ROWS, over // LANES, TILE_ROWS, LANES
    )
    up_tail = tiles.transpose(0, 2, 1, 3).reshape(gu_rows, over)
    up = jnp.concatenate([up_head, up_tail], axis=1)
    return gate, up, red[gu_rows + extra :]


def body(tokens, experts, gates, w_gate, w_up, w_down, cotangent):
    tok_rows, model_width = tokens.shape
    top_count = experts.shape[1]
    n_experts = lax.axis_size("ep")
    n_rep = lax.axis_size("rep")
    capacity = 3 * tok_rows * top_count // (2 * n_experts)
    pair_count = tok_rows * top_count
    gate_mat, up_mat, down_mat = (w_gate[0], w_up[0], w_down[0])
    ff_width = gate_mat.shape[1]
    slots = n_experts * capacity

    flat_exp = experts.reshape(pair_count)
    onehot = (flat_exp[:, None] == jnp.arange(n_experts, dtype=jnp.int32)[None, :]).astype(
        jnp.int32
    )
    slot_rank = jnp.sum((jnp.cumsum(onehot, axis=0) - onehot) * onehot, axis=1)
    slot_index = flat_exp * capacity + slot_rank
    source = jnp.zeros((slots,), jnp.int32).at[slot_index].set(
        jnp.arange(pair_count, dtype=jnp.int32)
    )
    filled = jnp.zeros((slots,), jnp.bfloat16).at[slot_index].set(1.0)
    token_src = source // top_count
    weights = gates.reshape(pair_count, 1).astype(jnp.float32)
    slot_weight = weights[source] * filled[:, None].astype(jnp.float32)
    scaled_rows = (slot_weight * cotangent[token_src].astype(jnp.float32)).astype(jnp.bfloat16)

    disp = jnp.concatenate(
        [tokens[token_src] * filled[:, None], scaled_rows], axis=1
    ).reshape(n_experts, capacity, 2 * model_width)
    recv = lax.all_to_all(disp, "ep", split_axis=0, concat_axis=0, tiled=True).reshape(
        slots, 2 * model_width
    )
    rows_in = recv[:, :model_width]
    out_grads = recv[:, model_width:]

    contract = (((1,), (1,)), ((), ()))
    rows_first = (((0,), (0,)), ((), ()))
    gate_pre = jnp.dot(rows_in, gate_mat, preferred_element_type=jnp.float32)
    up_pre = jnp.dot(rows_in, up_mat, preferred_element_type=jnp.float32)
    sigmoid_g = jax.nn.sigmoid(gate_pre)
    activated = gate_pre * sigmoid_g
    hidden = (activated * up_pre).astype(jnp.bfloat16)
    hidden_grad = lax.dot_general(out_grads, down_mat, contract, preferred_element_type=jnp.float32)
    gate_delta = (hidden_grad * up_pre * sigmoid_g * (1.0 + gate_pre * (1.0 - sigmoid_g))).astype(
        jnp.bfloat16
    )
    up_delta = (hidden_grad * activated).astype(jnp.bfloat16)

    gu_rows = model_width // n_rep
    packed = packed_weight_grads(recv, gate_delta, up_delta, hidden, n_rep)
    reduced = lax.optimization_barrier(
        lax.psum_scatter(packed, "rep", scatter_dimension=0, tiled=True)
    )[0]
    grad_gate, grad_up, grad_down = (
        part.astype(jnp.float32) for part in unpack_weight_grads(reduced, gu_rows, ff_width)
    )

    expert_out = jnp.dot(hidden, down_mat, preferred_element_type=jnp.float32).astype(jnp.bfloat16)
    row_grads = (
        lax.dot_general(gate_delta, gate_mat, contract, preferred_element_type=jnp.float32)
        + lax.dot_general(up_delta, up_mat, contract, preferred_element_type=jnp.float32)
    ).astype(jnp.bfloat16)
    back = jnp.concatenate([expert_out, row_grads], axis=1).reshape(
        n_experts, capacity, 2 * model_width
    )
    returned = lax.all_to_all(back, "ep", split_axis=0, concat_axis=0, tiled=True).reshape(
        slots, 2 * model_width
    )
    pair_back = returned[slot_index]
    pair_out = pair_back[:, :model_width]
    pair_grads = pair_back[:, model_width:]
    layer_out = jnp.sum(
        (weights * pair_out.astype(jnp.float32)).reshape(tok_rows, top_count, model_width), axis=1
    ).astype(jnp.bfloat16)
    gate_grads = jnp.einsum(
        "tkd,td->tk",
        pair_out.reshape(tok_rows, top_count, model_width),
        cotangent,
        preferred_element_type=jnp.float32,
    ).astype(jnp.bfloat16)
    input_grads = jnp.sum(
        pair_grads.astype(jnp.float32).reshape(tok_rows, top_count, model_width), axis=1
    ).astype(jnp.bfloat16)
    return (layer_out, input_grads, gate_grads, grad_gate[None], grad_up[None], grad_down[None])


def solution(mesh):
    in_specs = (
        P(("rep", "ep"), None),
        P(("rep", "ep"), None),
        P(("rep", "ep"), None),
        P("ep", None, None),
        P("ep", None, None),
        P("ep", None, None),
        P(("rep", "ep"), None),
    )
    out_specs = (
        P(("rep", "ep"), None),
        P(("rep", "ep"), None),
        P(("rep", "ep"), None),
        P("ep", "rep", None),
        P("ep", "rep", None),
        P("ep", "rep", None),
    )
    return jax.shard_map(body, mesh=mesh, in_specs=in_specs, out_specs=out_specs, check_vma=False)
```

```python
import jax
import jax.numpy as jnp
from jax import lax
from jax.experimental import pallas as pl
from jax.experimental.pallas import tpu as pltpu
from jax.sharding import PartitionSpec as P


TILE_ROWS = 16
LANES = 128


def _pack_kernel(x_ref, gd_ref, ud_ref, h_ref, og_ref, o_ref, down_ref):
    ff = gd_ref.shape[1]
    width = og_ref.shape[1]
    group, chunk, _ = o_ref.shape
    rows = x_ref.shape[1] // group
    down_rows = down_ref.shape[0] // (group * pl.num_programs(0))
    over = 2 * ff - width
    first = (((0,), (0,)), ((), ()))
    r = pl.program_id(0)

    @pl.when(r == 0)
    def _():
        down_ref[...] = lax.dot_general(
            h_ref[...], og_ref[...], first, preferred_element_type=jnp.float32
        )

    x = x_ref[...]
    g_all = lax.dot_general(x, gd_ref[...], first, preferred_element_type=jnp.float32)
    u_all = lax.dot_general(x, ud_ref[...], first, preferred_element_type=jnp.float32)
    col_tiles = over // LANES
    extra = rows * over // width
    for c in range(group):
        g = g_all[c * rows : (c + 1) * rows]
        u = u_all[c * rows : (c + 1) * rows]
        o_ref[c, :rows, :ff] = g.astype(o_ref.dtype)
        o_ref[c, :rows, ff:] = u[:, : width - ff].astype(o_ref.dtype)
        for i in range(rows // TILE_ROWS):
            for j in range(col_tiles):
                q, p = divmod(i * col_tiles + j, width // LANES)
                src = u[i * TILE_ROWS : (i + 1) * TILE_ROWS, width - ff + j * LANES :][:, :LANES]
                o_ref[
                    c, rows + q * TILE_ROWS : rows + (q + 1) * TILE_ROWS, p * LANES : (p + 1) * LANES
                ] = src.astype(o_ref.dtype)
        start = pl.multiple_of((r * group + c) * down_rows, 8)
        o_ref[c, rows + extra :, :] = down_ref[pl.ds(start, down_rows), :].astype(o_ref.dtype)


GROUP = 4


def packed_weight_grads(recv, gate_delta, up_delta, hidden, n_rep):
    slots, ff = gate_delta.shape
    model_width = recv.shape[1] // 2
    gu_rows = model_width // n_rep
    down_rows = ff // n_rep
    extra = gu_rows * (2 * ff - model_width) // model_width
    chunk = gu_rows + extra + down_rows
    flops = 2 * slots * (model_width * 2 * ff + ff * model_width)
    group = GROUP if n_rep % GROUP == 0 else 1
    return pl.pallas_call(
        _pack_kernel,
        grid=(n_rep // group,),
        in_specs=[
            pl.BlockSpec((slots, group * gu_rows), lambda r: (0, r)),
            pl.BlockSpec((slots, ff), lambda r: (0, 0)),
            pl.BlockSpec((slots, ff), lambda r: (0, 0)),
            pl.BlockSpec((slots, ff), lambda r: (0, 0)),
            pl.BlockSpec((slots, model_width), lambda r: (0, 1)),
        ],
        out_specs=pl.BlockSpec((group, chunk, model_width), lambda r: (r, 0, 0)),
        out_shape=jax.ShapeDtypeStruct((n_rep, chunk, model_width), jnp.bfloat16),
        scratch_shapes=[pltpu.VMEM((ff, model_width), jnp.float32)],
        compiler_params=pltpu.CompilerParams(dimension_semantics=("arbitrary",)),
        cost_estimate=pl.CostEstimate(
            flops=flops, transcendentals=0, bytes_accessed=2 * n_rep * chunk * model_width
        ),
    )(recv, gate_delta, up_delta, hidden, recv)


def unpack_weight_grads(red, gu_rows, ff):
    width = red.shape[1]
    over = 2 * ff - width
    extra = gu_rows * over // width
    gate = red[:gu_rows, :ff]
    up_head = red[:gu_rows, ff:]
    tiles = red[gu_rows : gu_rows + extra].reshape(
        extra // TILE_ROWS, TILE_ROWS, width // LANES, LANES
    )
    tiles = tiles.transpose(0, 2, 1, 3).reshape(
        gu_rows // TILE_ROWS, over // LANES, TILE_ROWS, LANES
    )
    up_tail = tiles.transpose(0, 2, 1, 3).reshape(gu_rows, over)
    up = jnp.concatenate([up_head, up_tail], axis=1)
    return gate, up, red[gu_rows + extra :]


def body(tokens, experts, gates, w_gate, w_up, w_down, cotangent):
    tok_rows, model_width = tokens.shape
    top_count = experts.shape[1]
    n_experts = lax.axis_size("ep")
    n_rep = lax.axis_size("rep")
    capacity = 3 * tok_rows * top_count // (2 * n_experts)
    pair_count = tok_rows * top_count
    gate_mat, up_mat, down_mat = (w_gate[0], w_up[0], w_down[0])
    ff_width = gate_mat.shape[1]
    slots = n_experts * capacity

    flat_exp = experts.reshape(pair_count)
    onehot = (flat_exp[:, None] == jnp.arange(n_experts, dtype=jnp.int32)[None, :]).astype(
        jnp.int32
    )
    slot_rank = jnp.sum((jnp.cumsum(onehot, axis=0) - onehot) * onehot, axis=1)
    slot_index = flat_exp * capacity + slot_rank
    source = jnp.zeros((slots,), jnp.int32).at[slot_index].set(
        jnp.arange(pair_count, dtype=jnp.int32)
    )
    filled = jnp.zeros((slots,), jnp.bfloat16).at[slot_index].set(1.0)
    token_src = source // top_count
    weights = gates.reshape(pair_count, 1).astype(jnp.float32)
    slot_weight = weights[source] * filled[:, None].astype(jnp.float32)
    scaled_rows = (slot_weight * cotangent[token_src].astype(jnp.float32)).astype(jnp.bfloat16)

    disp = jnp.concatenate(
        [tokens[token_src] * filled[:, None], scaled_rows], axis=1
    ).reshape(n_experts, capacity, 2 * model_width)
    recv = lax.all_to_all(disp, "ep", split_axis=0, concat_axis=0, tiled=True).reshape(
        slots, 2 * model_width
    )
    rows_in = recv[:, :model_width]
    out_grads = recv[:, model_width:]

    contract = (((1,), (1,)), ((), ()))
    rows_first = (((0,), (0,)), ((), ()))
    gate_pre = jnp.dot(rows_in, gate_mat, preferred_element_type=jnp.float32)
    up_pre = jnp.dot(rows_in, up_mat, preferred_element_type=jnp.float32)
    sigmoid_g = jax.nn.sigmoid(gate_pre)
    activated = gate_pre * sigmoid_g
    hidden = (activated * up_pre).astype(jnp.bfloat16)
    hidden_grad = lax.dot_general(out_grads, down_mat, contract, preferred_element_type=jnp.float32)
    gate_delta = (hidden_grad * up_pre * sigmoid_g * (1.0 + gate_pre * (1.0 - sigmoid_g))).astype(
        jnp.bfloat16
    )
    up_delta = (hidden_grad * activated).astype(jnp.bfloat16)

    gu_rows = model_width // n_rep
    packed = packed_weight_grads(recv, gate_delta, up_delta, hidden, n_rep)
    reduced = lax.optimization_barrier(
        lax.psum_scatter(packed, "rep", scatter_dimension=0, tiled=True)
    )[0]
    grad_gate, grad_up, grad_down = (
        part.astype(jnp.float32) for part in unpack_weight_grads(reduced, gu_rows, ff_width)
    )

    expert_out = jnp.dot(hidden, down_mat, preferred_element_type=jnp.float32).astype(jnp.bfloat16)
    row_grads = (
        lax.dot_general(gate_delta, gate_mat, contract, preferred_element_type=jnp.float32)
        + lax.dot_general(up_delta, up_mat, contract, preferred_element_type=jnp.float32)
    ).astype(jnp.bfloat16)
    back = jnp.concatenate([expert_out, row_grads], axis=1).reshape(
        n_experts, capacity, 2 * model_width
    )
    returned = lax.all_to_all(back, "ep", split_axis=0, concat_axis=0, tiled=True).reshape(
        slots, 2 * model_width
    )
    pair_back = returned[slot_index]
    pair_out = pair_back[:, :model_width]
    pair_grads = pair_back[:, model_width:]
    layer_out = jnp.sum(
        (weights * pair_out.astype(jnp.float32)).reshape(tok_rows, top_count, model_width), axis=1
    ).astype(jnp.bfloat16)
    gate_grads = jnp.einsum(
        "tkd,td->tk",
        pair_out.reshape(tok_rows, top_count, model_width),
        cotangent,
        preferred_element_type=jnp.float32,
    ).astype(jnp.bfloat16)
    input_grads = jnp.sum(
        pair_grads.astype(jnp.float32).reshape(tok_rows, top_count, model_width), axis=1
    ).astype(jnp.bfloat16)
    return (layer_out, input_grads, gate_grads, grad_gate[None], grad_up[None], grad_down[None])


def solution(mesh):
    in_specs = (
        P(("rep", "ep"), None),
        P(("rep", "ep"), None),
        P(("rep", "ep"), None),
        P("ep", None, None),
        P("ep", None, None),
        P("ep", None, None),
        P(("rep", "ep"), None),
    )
    out_specs = (
        P(("rep", "ep"), None),
        P(("rep", "ep"), None),
        P(("rep", "ep"), None),
        P("ep", "rep", None),
        P("ep", "rep", None),
        P("ep", "rep", None),
    )
    return jax.shard_map(body, mesh=mesh, in_specs=in_specs, out_specs=out_specs, check_vma=False)
```

```python
import jax
import jax.numpy as jnp
from jax import lax
from jax.experimental import pallas as pl
from jax.experimental.pallas import tpu as pltpu
from jax.sharding import PartitionSpec as P


TILE_ROWS = 16
LANES = 128


def _pack_kernel(x_ref, gd_ref, ud_ref, h_ref, og_ref, o_ref, down_ref):
    ff = gd_ref.shape[1]
    width = og_ref.shape[1]
    group, chunk, _ = o_ref.shape
    rows = x_ref.shape[1] // group
    down_rows = down_ref.shape[0] // (group * pl.num_programs(0))
    over = 2 * ff - width
    first = (((0,), (0,)), ((), ()))
    r = pl.program_id(0)

    @pl.when(r == 0)
    def _():
        down_ref[...] = lax.dot_general(
            h_ref[...], og_ref[...], first, preferred_element_type=jnp.float32
        )

    x = x_ref[...]
    g_all = lax.dot_general(x, gd_ref[...], first, preferred_element_type=jnp.float32)
    u_all = lax.dot_general(x, ud_ref[...], first, preferred_element_type=jnp.float32)
    col_tiles = over // LANES
    extra = rows * over // width
    for c in range(group):
        g = g_all[c * rows : (c + 1) * rows]
        u = u_all[c * rows : (c + 1) * rows]
        o_ref[c, :rows, :ff] = g.astype(o_ref.dtype)
        o_ref[c, :rows, ff:] = u[:, : width - ff].astype(o_ref.dtype)
        for i in range(rows // TILE_ROWS):
            for j in range(col_tiles):
                q, p = divmod(i * col_tiles + j, width // LANES)
                src = u[i * TILE_ROWS : (i + 1) * TILE_ROWS, width - ff + j * LANES :][:, :LANES]
                o_ref[
                    c, rows + q * TILE_ROWS : rows + (q + 1) * TILE_ROWS, p * LANES : (p + 1) * LANES
                ] = src.astype(o_ref.dtype)
        start = pl.multiple_of((r * group + c) * down_rows, 8)
        o_ref[c, rows + extra :, :] = down_ref[pl.ds(start, down_rows), :].astype(o_ref.dtype)


GROUP = 4


def packed_weight_grads(rows_in, gate_delta, up_delta, hidden, out_grads, n_rep):
    slots, ff = gate_delta.shape
    model_width = rows_in.shape[1]
    gu_rows = model_width // n_rep
    down_rows = ff // n_rep
    extra = gu_rows * (2 * ff - model_width) // model_width
    chunk = gu_rows + extra + down_rows
    flops = 2 * slots * (model_width * 2 * ff + ff * model_width)
    group = GROUP if n_rep % GROUP == 0 else 1
    return pl.pallas_call(
        _pack_kernel,
        grid=(n_rep // group,),
        in_specs=[
            pl.BlockSpec((slots, group * gu_rows), lambda r: (0, r)),
            pl.BlockSpec((slots, ff), lambda r: (0, 0)),
            pl.BlockSpec((slots, ff), lambda r: (0, 0)),
            pl.BlockSpec((slots, ff), lambda r: (0, 0)),
            pl.BlockSpec((slots, model_width), lambda r: (0, 0)),
        ],
        out_specs=pl.BlockSpec((group, chunk, model_width), lambda r: (r, 0, 0)),
        out_shape=jax.ShapeDtypeStruct((n_rep, chunk, model_width), jnp.bfloat16),
        scratch_shapes=[pltpu.VMEM((ff, model_width), jnp.float32)],
        compiler_params=pltpu.CompilerParams(dimension_semantics=("arbitrary",)),
        cost_estimate=pl.CostEstimate(
            flops=flops, transcendentals=0, bytes_accessed=2 * n_rep * chunk * model_width
        ),
    )(rows_in, gate_delta, up_delta, hidden, out_grads)


def unpack_weight_grads(red, gu_rows, ff):
    width = red.shape[1]
    over = 2 * ff - width
    extra = gu_rows * over // width
    gate = red[:gu_rows, :ff]
    up_head = red[:gu_rows, ff:]
    tiles = red[gu_rows : gu_rows + extra].reshape(
        extra // TILE_ROWS, TILE_ROWS, width // LANES, LANES
    )
    tiles = tiles.transpose(0, 2, 1, 3).reshape(
        gu_rows // TILE_ROWS, over // LANES, TILE_ROWS, LANES
    )
    up_tail = tiles.transpose(0, 2, 1, 3).reshape(gu_rows, over)
    up = jnp.concatenate([up_head, up_tail], axis=1)
    return gate, up, red[gu_rows + extra :]


def body(tokens, experts, gates, w_gate, w_up, w_down, cotangent):
    tok_rows, model_width = tokens.shape
    top_count = experts.shape[1]
    n_experts = lax.axis_size("ep")
    n_rep = lax.axis_size("rep")
    capacity = 3 * tok_rows * top_count // (2 * n_experts)
    pair_count = tok_rows * top_count
    gate_mat, up_mat, down_mat = (w_gate[0], w_up[0], w_down[0])
    ff_width = gate_mat.shape[1]
    slots = n_experts * capacity

    flat_exp = experts.reshape(pair_count)
    onehot = (flat_exp[:, None] == jnp.arange(n_experts, dtype=jnp.int32)[None, :]).astype(
        jnp.int32
    )
    slot_rank = jnp.sum((jnp.cumsum(onehot, axis=0) - onehot) * onehot, axis=1)
    slot_index = flat_exp * capacity + slot_rank
    source = jnp.zeros((slots,), jnp.int32).at[slot_index].set(
        jnp.arange(pair_count, dtype=jnp.int32)
    )
    filled = jnp.zeros((slots,), jnp.bfloat16).at[slot_index].set(1.0)
    token_src = source // top_count
    weights = gates.reshape(pair_count, 1).astype(jnp.float32)
    slot_weight = weights[source] * filled[:, None].astype(jnp.float32)
    scaled_rows = (slot_weight * cotangent[token_src].astype(jnp.float32)).astype(jnp.bfloat16)

    tok_disp = (tokens[token_src] * filled[:, None]).reshape(n_experts, capacity, model_width)
    rows_in = lax.all_to_all(tok_disp, "ep", split_axis=0, concat_axis=0, tiled=True).reshape(
        slots, model_width
    )
    grad_disp = scaled_rows.reshape(n_experts, capacity, model_width)
    out_grads = lax.all_to_all(grad_disp, "ep", split_axis=0, concat_axis=0, tiled=True).reshape(
        slots, model_width
    )

    contract = (((1,), (1,)), ((), ()))
    rows_first = (((0,), (0,)), ((), ()))
    gate_pre = jnp.dot(rows_in, gate_mat, preferred_element_type=jnp.float32)
    up_pre = jnp.dot(rows_in, up_mat, preferred_element_type=jnp.float32)
    sigmoid_g = jax.nn.sigmoid(gate_pre)
    activated = gate_pre * sigmoid_g
    hidden = (activated * up_pre).astype(jnp.bfloat16)
    hidden_grad = lax.dot_general(out_grads, down_mat, contract, preferred_element_type=jnp.float32)
    gate_delta = (hidden_grad * up_pre * sigmoid_g * (1.0 + gate_pre * (1.0 - sigmoid_g))).astype(
        jnp.bfloat16
    )
    up_delta = (hidden_grad * activated).astype(jnp.bfloat16)

    gu_rows = model_width // n_rep
    packed = packed_weight_grads(rows_in, gate_delta, up_delta, hidden, out_grads, n_rep)
    reduced = lax.optimization_barrier(
        lax.psum_scatter(packed, "rep", scatter_dimension=0, tiled=True)
    )[0]
    grad_gate, grad_up, grad_down = (
        part.astype(jnp.float32) for part in unpack_weight_grads(reduced, gu_rows, ff_width)
    )

    expert_out = jnp.dot(hidden, down_mat, preferred_element_type=jnp.float32).astype(jnp.bfloat16)
    row_grads = (
        lax.dot_general(gate_delta, gate_mat, contract, preferred_element_type=jnp.float32)
        + lax.dot_general(up_delta, up_mat, contract, preferred_element_type=jnp.float32)
    ).astype(jnp.bfloat16)
    back = jnp.concatenate([expert_out, row_grads], axis=1).reshape(
        n_experts, capacity, 2 * model_width
    )
    returned = lax.all_to_all(back, "ep", split_axis=0, concat_axis=0, tiled=True).reshape(
        slots, 2 * model_width
    )
    pair_back = returned[slot_index]
    pair_out = pair_back[:, :model_width]
    pair_grads = pair_back[:, model_width:]
    layer_out = jnp.sum(
        (weights * pair_out.astype(jnp.float32)).reshape(tok_rows, top_count, model_width), axis=1
    ).astype(jnp.bfloat16)
    gate_grads = jnp.einsum(
        "tkd,td->tk",
        pair_out.reshape(tok_rows, top_count, model_width),
        cotangent,
        preferred_element_type=jnp.float32,
    ).astype(jnp.bfloat16)
    input_grads = jnp.sum(
        pair_grads.astype(jnp.float32).reshape(tok_rows, top_count, model_width), axis=1
    ).astype(jnp.bfloat16)
    return (layer_out, input_grads, gate_grads, grad_gate[None], grad_up[None], grad_down[None])


def solution(mesh):
    in_specs = (
        P(("rep", "ep"), None),
        P(("rep", "ep"), None),
        P(("rep", "ep"), None),
        P("ep", None, None),
        P("ep", None, None),
        P("ep", None, None),
        P(("rep", "ep"), None),
    )
    out_specs = (
        P(("rep", "ep"), None),
        P(("rep", "ep"), None),
        P(("rep", "ep"), None),
        P("ep", "rep", None),
        P("ep", "rep", None),
        P("ep", "rep", None),
    )
    return jax.shard_map(body, mesh=mesh, in_specs=in_specs, out_specs=out_specs, check_vma=False)
```

```python
import jax
import jax.numpy as jnp
from jax import lax
from jax.experimental import pallas as pl
from jax.experimental.pallas import tpu as pltpu
from jax.sharding import PartitionSpec as P


TILE_ROWS = 16
LANES = 128


def _pack_kernel(x_ref, gd_ref, ud_ref, h_ref, og_ref, o_ref, down_ref):
    ff = gd_ref.shape[1]
    width = og_ref.shape[1]
    group, chunk, _ = o_ref.shape
    rows = x_ref.shape[1] // group
    down_rows = down_ref.shape[0] // (group * pl.num_programs(0))
    over = 2 * ff - width
    first = (((0,), (0,)), ((), ()))
    r = pl.program_id(0)

    @pl.when(r == 0)
    def _():
        down_ref[...] = lax.dot_general(
            h_ref[...], og_ref[...], first, preferred_element_type=jnp.float32
        )

    x = x_ref[...]
    g_all = lax.dot_general(x, gd_ref[...], first, preferred_element_type=jnp.float32)
    u_all = lax.dot_general(x, ud_ref[...], first, preferred_element_type=jnp.float32)
    col_tiles = over // LANES
    extra = rows * over // width
    for c in range(group):
        g = g_all[c * rows : (c + 1) * rows]
        u = u_all[c * rows : (c + 1) * rows]
        o_ref[c, :rows, :ff] = g.astype(o_ref.dtype)
        o_ref[c, :rows, ff:] = u[:, : width - ff].astype(o_ref.dtype)
        for i in range(rows // TILE_ROWS):
            for j in range(col_tiles):
                q, p = divmod(i * col_tiles + j, width // LANES)
                src = u[i * TILE_ROWS : (i + 1) * TILE_ROWS, width - ff + j * LANES :][:, :LANES]
                o_ref[
                    c, rows + q * TILE_ROWS : rows + (q + 1) * TILE_ROWS, p * LANES : (p + 1) * LANES
                ] = src.astype(o_ref.dtype)
        start = pl.multiple_of((r * group + c) * down_rows, 8)
        o_ref[c, rows + extra :, :] = down_ref[pl.ds(start, down_rows), :].astype(o_ref.dtype)


GROUP = 4


def packed_weight_grads(recv, gate_delta, up_delta, hidden, n_rep):
    slots, ff = gate_delta.shape
    model_width = recv.shape[1] // 2
    gu_rows = model_width // n_rep
    down_rows = ff // n_rep
    extra = gu_rows * (2 * ff - model_width) // model_width
    chunk = gu_rows + extra + down_rows
    flops = 2 * slots * (model_width * 2 * ff + ff * model_width)
    group = GROUP if n_rep % GROUP == 0 else 1
    return pl.pallas_call(
        _pack_kernel,
        grid=(n_rep // group,),
        in_specs=[
            pl.BlockSpec((slots, group * gu_rows), lambda r: (0, r)),
            pl.BlockSpec((slots, ff), lambda r: (0, 0)),
            pl.BlockSpec((slots, ff), lambda r: (0, 0)),
            pl.BlockSpec((slots, ff), lambda r: (0, 0)),
            pl.BlockSpec((slots, model_width), lambda r: (0, 1)),
        ],
        out_specs=pl.BlockSpec((group, chunk, model_width), lambda r: (r, 0, 0)),
        out_shape=jax.ShapeDtypeStruct((n_rep, chunk, model_width), jnp.bfloat16),
        scratch_shapes=[pltpu.VMEM((ff, model_width), jnp.float32)],
        compiler_params=pltpu.CompilerParams(dimension_semantics=("arbitrary",)),
        cost_estimate=pl.CostEstimate(
            flops=flops, transcendentals=0, bytes_accessed=2 * n_rep * chunk * model_width
        ),
    )(recv, gate_delta, up_delta, hidden, recv)


def unpack_weight_grads(red, gu_rows, ff):
    width = red.shape[1]
    over = 2 * ff - width
    extra = gu_rows * over // width
    gate = red[:gu_rows, :ff]
    up_head = red[:gu_rows, ff:]
    tiles = red[gu_rows : gu_rows + extra].reshape(
        extra // TILE_ROWS, TILE_ROWS, width // LANES, LANES
    )
    tiles = tiles.transpose(0, 2, 1, 3).reshape(
        gu_rows // TILE_ROWS, over // LANES, TILE_ROWS, LANES
    )
    up_tail = tiles.transpose(0, 2, 1, 3).reshape(gu_rows, over)
    up = jnp.concatenate([up_head, up_tail], axis=1)
    return gate, up, red[gu_rows + extra :]


def body(tokens, experts, gates, w_gate, w_up, w_down, cotangent):
    tok_rows, model_width = tokens.shape
    top_count = experts.shape[1]
    n_experts = lax.axis_size("ep")
    n_rep = lax.axis_size("rep")
    capacity = 3 * tok_rows * top_count // (2 * n_experts)
    pair_count = tok_rows * top_count
    gate_mat, up_mat, down_mat = (w_gate[0], w_up[0], w_down[0])
    ff_width = gate_mat.shape[1]
    slots = n_experts * capacity

    flat_exp = experts.reshape(pair_count)
    onehot = (flat_exp[:, None] == jnp.arange(n_experts, dtype=jnp.int32)[None, :]).astype(
        jnp.int32
    )
    slot_rank = jnp.sum((jnp.cumsum(onehot, axis=0) - onehot) * onehot, axis=1)
    slot_index = flat_exp * capacity + slot_rank
    hit = (
        slot_index.reshape(tok_rows, top_count, 1)
        == jnp.arange(slots, dtype=jnp.int32)[None, None, :]
    )
    select = jnp.sum(hit, axis=1).astype(jnp.bfloat16)
    gate_select = jnp.sum(jnp.where(hit, gates[:, :, None], 0), axis=1).astype(jnp.bfloat16)
    rows_first = (((0,), (0,)), ((), ()))
    tok_rows_out = lax.dot_general(select, tokens, rows_first, preferred_element_type=jnp.float32)
    scaled_rows = lax.dot_general(
        gate_select, cotangent, rows_first, preferred_element_type=jnp.float32
    )
    weights = gates.reshape(pair_count, 1).astype(jnp.float32)

    disp = jnp.concatenate(
        [tok_rows_out.astype(jnp.bfloat16), scaled_rows.astype(jnp.bfloat16)], axis=1
    ).reshape(n_experts, capacity, 2 * model_width)
    recv = lax.all_to_all(disp, "ep", split_axis=0, concat_axis=0, tiled=True).reshape(
        slots, 2 * model_width
    )
    rows_in = recv[:, :model_width]
    out_grads = recv[:, model_width:]

    contract = (((1,), (1,)), ((), ()))
    gate_pre = jnp.dot(rows_in, gate_mat, preferred_element_type=jnp.float32)
    up_pre = jnp.dot(rows_in, up_mat, preferred_element_type=jnp.float32)
    sigmoid_g = jax.nn.sigmoid(gate_pre)
    activated = gate_pre * sigmoid_g
    hidden = (activated * up_pre).astype(jnp.bfloat16)
    hidden_grad = lax.dot_general(out_grads, down_mat, contract, preferred_element_type=jnp.float32)
    gate_delta = (hidden_grad * up_pre * sigmoid_g * (1.0 + gate_pre * (1.0 - sigmoid_g))).astype(
        jnp.bfloat16
    )
    up_delta = (hidden_grad * activated).astype(jnp.bfloat16)

    gu_rows = model_width // n_rep
    packed = packed_weight_grads(recv, gate_delta, up_delta, hidden, n_rep)
    reduced = lax.optimization_barrier(
        lax.psum_scatter(packed, "rep", scatter_dimension=0, tiled=True)
    )[0]
    grad_gate, grad_up, grad_down = (
        part.astype(jnp.float32) for part in unpack_weight_grads(reduced, gu_rows, ff_width)
    )

    expert_out = jnp.dot(hidden, down_mat, preferred_element_type=jnp.float32).astype(jnp.bfloat16)
    row_grads = (
        lax.dot_general(gate_delta, gate_mat, contract, preferred_element_type=jnp.float32)
        + lax.dot_general(up_delta, up_mat, contract, preferred_element_type=jnp.float32)
    ).astype(jnp.bfloat16)
    back = jnp.concatenate([expert_out, row_grads], axis=1).reshape(
        n_experts, capacity, 2 * model_width
    )
    returned = lax.all_to_all(back, "ep", split_axis=0, concat_axis=0, tiled=True).reshape(
        slots, 2 * model_width
    )
    pair_back = returned[slot_index]
    pair_out = pair_back[:, :model_width]
    pair_grads = pair_back[:, model_width:]
    layer_out = jnp.sum(
        (weights * pair_out.astype(jnp.float32)).reshape(tok_rows, top_count, model_width), axis=1
    ).astype(jnp.bfloat16)
    gate_grads = jnp.einsum(
        "tkd,td->tk",
        pair_out.reshape(tok_rows, top_count, model_width),
        cotangent,
        preferred_element_type=jnp.float32,
    ).astype(jnp.bfloat16)
    input_grads = jnp.sum(
        pair_grads.astype(jnp.float32).reshape(tok_rows, top_count, model_width), axis=1
    ).astype(jnp.bfloat16)
    return (layer_out, input_grads, gate_grads, grad_gate[None], grad_up[None], grad_down[None])


def solution(mesh):
    in_specs = (
        P(("rep", "ep"), None),
        P(("rep", "ep"), None),
        P(("rep", "ep"), None),
        P("ep", None, None),
        P("ep", None, None),
        P("ep", None, None),
        P(("rep", "ep"), None),
    )
    out_specs = (
        P(("rep", "ep"), None),
        P(("rep", "ep"), None),
        P(("rep", "ep"), None),
        P("ep", "rep", None),
        P("ep", "rep", None),
        P("ep", "rep", None),
    )
    return jax.shard_map(body, mesh=mesh, in_specs=in_specs, out_specs=out_specs, check_vma=False)
```

```python
import jax
import jax.numpy as jnp
from jax import lax
from jax.experimental import pallas as pl
from jax.experimental.pallas import tpu as pltpu
from jax.sharding import PartitionSpec as P


TILE_ROWS = 16
LANES = 128


def _pack_kernel(x_ref, gd_ref, ud_ref, h_ref, og_ref, o_ref, down_ref):
    ff = gd_ref.shape[1]
    width = og_ref.shape[1]
    group, chunk, _ = o_ref.shape
    rows = x_ref.shape[1] // group
    down_rows = down_ref.shape[0] // (group * pl.num_programs(0))
    over = 2 * ff - width
    first = (((0,), (0,)), ((), ()))
    r = pl.program_id(0)

    @pl.when(r == 0)
    def _():
        down_ref[...] = lax.dot_general(
            h_ref[...], og_ref[...], first, preferred_element_type=jnp.float32
        )

    x = x_ref[...]
    g_all = lax.dot_general(x, gd_ref[...], first, preferred_element_type=jnp.float32)
    u_all = lax.dot_general(x, ud_ref[...], first, preferred_element_type=jnp.float32)
    col_tiles = over // LANES
    extra = rows * over // width
    for c in range(group):
        g = g_all[c * rows : (c + 1) * rows]
        u = u_all[c * rows : (c + 1) * rows]
        o_ref[c, :rows, :ff] = g.astype(o_ref.dtype)
        o_ref[c, :rows, ff:] = u[:, : width - ff].astype(o_ref.dtype)
        for i in range(rows // TILE_ROWS):
            for j in range(col_tiles):
                q, p = divmod(i * col_tiles + j, width // LANES)
                src = u[i * TILE_ROWS : (i + 1) * TILE_ROWS, width - ff + j * LANES :][:, :LANES]
                o_ref[
                    c, rows + q * TILE_ROWS : rows + (q + 1) * TILE_ROWS, p * LANES : (p + 1) * LANES
                ] = src.astype(o_ref.dtype)
        start = pl.multiple_of((r * group + c) * down_rows, 8)
        o_ref[c, rows + extra :, :] = down_ref[pl.ds(start, down_rows), :].astype(o_ref.dtype)


GROUP = 8


def packed_weight_grads(recv, gate_delta, up_delta, hidden, n_rep):
    slots, ff = gate_delta.shape
    model_width = recv.shape[1] // 2
    gu_rows = model_width // n_rep
    down_rows = ff // n_rep
    extra = gu_rows * (2 * ff - model_width) // model_width
    chunk = gu_rows + extra + down_rows
    flops = 2 * slots * (model_width * 2 * ff + ff * model_width)
    group = GROUP if n_rep % GROUP == 0 else 1
    return pl.pallas_call(
        _pack_kernel,
        grid=(n_rep // group,),
        in_specs=[
            pl.BlockSpec((slots, group * gu_rows), lambda r: (0, r)),
            pl.BlockSpec((slots, ff), lambda r: (0, 0)),
            pl.BlockSpec((slots, ff), lambda r: (0, 0)),
            pl.BlockSpec((slots, ff), lambda r: (0, 0)),
            pl.BlockSpec((slots, model_width), lambda r: (0, 1)),
        ],
        out_specs=pl.BlockSpec((group, chunk, model_width), lambda r: (r, 0, 0)),
        out_shape=jax.ShapeDtypeStruct((n_rep, chunk, model_width), jnp.bfloat16),
        scratch_shapes=[pltpu.VMEM((ff, model_width), jnp.float32)],
        compiler_params=pltpu.CompilerParams(dimension_semantics=("arbitrary",)),
        cost_estimate=pl.CostEstimate(
            flops=flops, transcendentals=0, bytes_accessed=2 * n_rep * chunk * model_width
        ),
    )(recv, gate_delta, up_delta, hidden, recv)


def unpack_weight_grads(red, gu_rows, ff):
    width = red.shape[1]
    over = 2 * ff - width
    extra = gu_rows * over // width
    gate = red[:gu_rows, :ff]
    up_head = red[:gu_rows, ff:]
    tiles = red[gu_rows : gu_rows + extra].reshape(
        extra // TILE_ROWS, TILE_ROWS, width // LANES, LANES
    )
    tiles = tiles.transpose(0, 2, 1, 3).reshape(
        gu_rows // TILE_ROWS, over // LANES, TILE_ROWS, LANES
    )
    up_tail = tiles.transpose(0, 2, 1, 3).reshape(gu_rows, over)
    up = jnp.concatenate([up_head, up_tail], axis=1)
    return gate, up, red[gu_rows + extra :]


def body(tokens, experts, gates, w_gate, w_up, w_down, cotangent):
    tok_rows, model_width = tokens.shape
    top_count = experts.shape[1]
    n_experts = lax.axis_size("ep")
    n_rep = lax.axis_size("rep")
    capacity = 3 * tok_rows * top_count // (2 * n_experts)
    pair_count = tok_rows * top_count
    gate_mat, up_mat, down_mat = (w_gate[0], w_up[0], w_down[0])
    ff_width = gate_mat.shape[1]
    slots = n_experts * capacity

    flat_exp = experts.reshape(pair_count)
    onehot = (flat_exp[:, None] == jnp.arange(n_experts, dtype=jnp.int32)[None, :]).astype(
        jnp.int32
    )
    slot_rank = jnp.sum((jnp.cumsum(onehot, axis=0) - onehot) * onehot, axis=1)
    slot_index = flat_exp * capacity + slot_rank
    hit = (
        slot_index.reshape(tok_rows, top_count, 1)
        == jnp.arange(slots, dtype=jnp.int32)[None, None, :]
    )
    select = jnp.sum(hit, axis=1).astype(jnp.bfloat16)
    gate_select = jnp.sum(jnp.where(hit, gates[:, :, None], 0), axis=1).astype(jnp.bfloat16)
    rows_first = (((0,), (0,)), ((), ()))
    tok_rows_out = lax.dot_general(select, tokens, rows_first, preferred_element_type=jnp.float32)
    scaled_rows = lax.dot_general(
        gate_select, cotangent, rows_first, preferred_element_type=jnp.float32
    )
    weights = gates.reshape(pair_count, 1).astype(jnp.float32)

    disp = jnp.concatenate(
        [tok_rows_out.astype(jnp.bfloat16), scaled_rows.astype(jnp.bfloat16)], axis=1
    ).reshape(n_experts, capacity, 2 * model_width)
    recv = lax.all_to_all(disp, "ep", split_axis=0, concat_axis=0, tiled=True).reshape(
        slots, 2 * model_width
    )
    rows_in = recv[:, :model_width]
    out_grads = recv[:, model_width:]

    contract = (((1,), (1,)), ((), ()))
    gate_pre = jnp.dot(rows_in, gate_mat, preferred_element_type=jnp.float32)
    up_pre = jnp.dot(rows_in, up_mat, preferred_element_type=jnp.float32)
    sigmoid_g = jax.nn.sigmoid(gate_pre)
    activated = gate_pre * sigmoid_g
    hidden = (activated * up_pre).astype(jnp.bfloat16)
    hidden_grad = lax.dot_general(out_grads, down_mat, contract, preferred_element_type=jnp.float32)
    gate_delta = (hidden_grad * up_pre * sigmoid_g * (1.0 + gate_pre * (1.0 - sigmoid_g))).astype(
        jnp.bfloat16
    )
    up_delta = (hidden_grad * activated).astype(jnp.bfloat16)

    gu_rows = model_width // n_rep
    packed = packed_weight_grads(recv, gate_delta, up_delta, hidden, n_rep)
    reduced = lax.optimization_barrier(
        lax.psum_scatter(packed, "rep", scatter_dimension=0, tiled=True)
    )[0]
    grad_gate, grad_up, grad_down = (
        part.astype(jnp.float32) for part in unpack_weight_grads(reduced, gu_rows, ff_width)
    )

    expert_out = jnp.dot(hidden, down_mat, preferred_element_type=jnp.float32).astype(jnp.bfloat16)
    row_grads = (
        lax.dot_general(gate_delta, gate_mat, contract, preferred_element_type=jnp.float32)
        + lax.dot_general(up_delta, up_mat, contract, preferred_element_type=jnp.float32)
    ).astype(jnp.bfloat16)
    back = jnp.concatenate([expert_out, row_grads], axis=1).reshape(
        n_experts, capacity, 2 * model_width
    )
    returned = lax.all_to_all(back, "ep", split_axis=0, concat_axis=0, tiled=True).reshape(
        slots, 2 * model_width
    )
    pair_back = returned[slot_index]
    pair_out = pair_back[:, :model_width]
    pair_grads = pair_back[:, model_width:]
    layer_out = jnp.sum(
        (weights * pair_out.astype(jnp.float32)).reshape(tok_rows, top_count, model_width), axis=1
    ).astype(jnp.bfloat16)
    gate_grads = jnp.einsum(
        "tkd,td->tk",
        pair_out.reshape(tok_rows, top_count, model_width),
        cotangent,
        preferred_element_type=jnp.float32,
    ).astype(jnp.bfloat16)
    input_grads = jnp.sum(
        pair_grads.astype(jnp.float32).reshape(tok_rows, top_count, model_width), axis=1
    ).astype(jnp.bfloat16)
    return (layer_out, input_grads, gate_grads, grad_gate[None], grad_up[None], grad_down[None])


def solution(mesh):
    in_specs = (
        P(("rep", "ep"), None),
        P(("rep", "ep"), None),
        P(("rep", "ep"), None),
        P("ep", None, None),
        P("ep", None, None),
        P("ep", None, None),
        P(("rep", "ep"), None),
    )
    out_specs = (
        P(("rep", "ep"), None),
        P(("rep", "ep"), None),
        P(("rep", "ep"), None),
        P("ep", "rep", None),
        P("ep", "rep", None),
        P("ep", "rep", None),
    )
    return jax.shard_map(body, mesh=mesh, in_specs=in_specs, out_specs=out_specs, check_vma=False)
```

```python
import jax
import jax.numpy as jnp
from jax import lax
from jax.experimental import pallas as pl
from jax.experimental.pallas import tpu as pltpu
from jax.sharding import PartitionSpec as P


TILE_ROWS = 16
LANES = 128


def _pack_kernel(x_ref, gd_ref, ud_ref, h_ref, og_ref, o_ref, down_ref):
    ff = gd_ref.shape[1]
    width = og_ref.shape[1]
    group, chunk, _ = o_ref.shape
    rows = x_ref.shape[1] // group
    down_rows = down_ref.shape[0] // (group * pl.num_programs(0))
    over = 2 * ff - width
    first = (((0,), (0,)), ((), ()))
    r = pl.program_id(0)

    @pl.when(r == 0)
    def _():
        down_ref[...] = lax.dot_general(
            h_ref[...], og_ref[...], first, preferred_element_type=jnp.float32
        )

    x = x_ref[...]
    g_all = lax.dot_general(x, gd_ref[...], first, preferred_element_type=jnp.float32)
    u_all = lax.dot_general(x, ud_ref[...], first, preferred_element_type=jnp.float32)
    col_tiles = over // LANES
    extra = rows * over // width
    for c in range(group):
        g = g_all[c * rows : (c + 1) * rows]
        u = u_all[c * rows : (c + 1) * rows]
        o_ref[c, :rows, :ff] = g.astype(o_ref.dtype)
        o_ref[c, :rows, ff:] = u[:, : width - ff].astype(o_ref.dtype)
        for i in range(rows // TILE_ROWS):
            for j in range(col_tiles):
                q, p = divmod(i * col_tiles + j, width // LANES)
                src = u[i * TILE_ROWS : (i + 1) * TILE_ROWS, width - ff + j * LANES :][:, :LANES]
                o_ref[
                    c, rows + q * TILE_ROWS : rows + (q + 1) * TILE_ROWS, p * LANES : (p + 1) * LANES
                ] = src.astype(o_ref.dtype)
        start = pl.multiple_of((r * group + c) * down_rows, 8)
        o_ref[c, rows + extra :, :] = down_ref[pl.ds(start, down_rows), :].astype(o_ref.dtype)


GROUP = 4


def packed_weight_grads(recv, gate_delta, up_delta, hidden, n_rep):
    slots, ff = gate_delta.shape
    model_width = recv.shape[1] // 2
    gu_rows = model_width // n_rep
    down_rows = ff // n_rep
    extra = gu_rows * (2 * ff - model_width) // model_width
    chunk = gu_rows + extra + down_rows
    flops = 2 * slots * (model_width * 2 * ff + ff * model_width)
    group = GROUP if n_rep % GROUP == 0 else 1
    return pl.pallas_call(
        _pack_kernel,
        grid=(n_rep // group,),
        in_specs=[
            pl.BlockSpec((slots, group * gu_rows), lambda r: (0, r)),
            pl.BlockSpec((slots, ff), lambda r: (0, 0)),
            pl.BlockSpec((slots, ff), lambda r: (0, 0)),
            pl.BlockSpec((slots, ff), lambda r: (0, 0)),
            pl.BlockSpec((slots, model_width), lambda r: (0, 1)),
        ],
        out_specs=pl.BlockSpec((group, chunk, model_width), lambda r: (r, 0, 0)),
        out_shape=jax.ShapeDtypeStruct((n_rep, chunk, model_width), jnp.bfloat16),
        scratch_shapes=[pltpu.VMEM((ff, model_width), jnp.float32)],
        compiler_params=pltpu.CompilerParams(dimension_semantics=("arbitrary",)),
        cost_estimate=pl.CostEstimate(
            flops=flops, transcendentals=0, bytes_accessed=2 * n_rep * chunk * model_width
        ),
    )(recv, gate_delta, up_delta, hidden, recv)


def _unpack_kernel(red_ref, g_ref, u_ref, d_ref):
    rows, ff = g_ref.shape
    width = red_ref.shape[2]
    over = 2 * ff - width
    extra = rows * over // width
    g_ref[...] = red_ref[0, :rows, :ff].astype(g_ref.dtype)
    u_ref[:, : width - ff] = red_ref[0, :rows, ff:].astype(u_ref.dtype)
    col_tiles = over // LANES
    for i in range(rows // TILE_ROWS):
        for j in range(col_tiles):
            q, p = divmod(i * col_tiles + j, width // LANES)
            col = width - ff + j * LANES
            u_ref[i * TILE_ROWS : (i + 1) * TILE_ROWS, col : col + LANES] = red_ref[
                0, rows + q * TILE_ROWS : rows + (q + 1) * TILE_ROWS, p * LANES : (p + 1) * LANES
            ].astype(u_ref.dtype)
    d_ref[...] = red_ref[0, rows + extra :, :].astype(d_ref.dtype)


def unpack_weight_grads(red, gu_rows, ff):
    _, chunk, width = red.shape
    extra = gu_rows * (2 * ff - width) // width
    return pl.pallas_call(
        _unpack_kernel,
        out_shape=(
            jax.ShapeDtypeStruct((gu_rows, ff), jnp.float32),
            jax.ShapeDtypeStruct((gu_rows, ff), jnp.float32),
            jax.ShapeDtypeStruct((chunk - gu_rows - extra, width), jnp.float32),
        ),
    )(red)


def body(tokens, experts, gates, w_gate, w_up, w_down, cotangent):
    tok_rows, model_width = tokens.shape
    top_count = experts.shape[1]
    n_experts = lax.axis_size("ep")
    n_rep = lax.axis_size("rep")
    capacity = 3 * tok_rows * top_count // (2 * n_experts)
    pair_count = tok_rows * top_count
    gate_mat, up_mat, down_mat = (w_gate[0], w_up[0], w_down[0])
    ff_width = gate_mat.shape[1]
    slots = n_experts * capacity

    flat_exp = experts.reshape(pair_count)
    onehot = (flat_exp[:, None] == jnp.arange(n_experts, dtype=jnp.int32)[None, :]).astype(
        jnp.int32
    )
    slot_rank = jnp.sum((jnp.cumsum(onehot, axis=0) - onehot) * onehot, axis=1)
    slot_index = flat_exp * capacity + slot_rank
    hit = (
        slot_index.reshape(tok_rows, top_count, 1)
        == jnp.arange(slots, dtype=jnp.int32)[None, None, :]
    )
    select = jnp.sum(hit, axis=1).astype(jnp.bfloat16)
    gate_select = jnp.sum(jnp.where(hit, gates[:, :, None], 0), axis=1).astype(jnp.bfloat16)
    rows_first = (((0,), (0,)), ((), ()))
    tok_rows_out = lax.dot_general(select, tokens, rows_first, preferred_element_type=jnp.float32)
    scaled_rows = lax.dot_general(
        gate_select, cotangent, rows_first, preferred_element_type=jnp.float32
    )
    weights = gates.reshape(pair_count, 1).astype(jnp.float32)

    disp = jnp.concatenate(
        [tok_rows_out.astype(jnp.bfloat16), scaled_rows.astype(jnp.bfloat16)], axis=1
    ).reshape(n_experts, capacity, 2 * model_width)
    recv = lax.all_to_all(disp, "ep", split_axis=0, concat_axis=0, tiled=True).reshape(
        slots, 2 * model_width
    )
    rows_in = recv[:, :model_width]
    out_grads = recv[:, model_width:]

    contract = (((1,), (1,)), ((), ()))
    gate_pre = jnp.dot(rows_in, gate_mat, preferred_element_type=jnp.float32)
    up_pre = jnp.dot(rows_in, up_mat, preferred_element_type=jnp.float32)
    sigmoid_g = jax.nn.sigmoid(gate_pre)
    activated = gate_pre * sigmoid_g
    hidden = (activated * up_pre).astype(jnp.bfloat16)
    hidden_grad = lax.dot_general(out_grads, down_mat, contract, preferred_element_type=jnp.float32)
    gate_delta = (hidden_grad * up_pre * sigmoid_g * (1.0 + gate_pre * (1.0 - sigmoid_g))).astype(
        jnp.bfloat16
    )
    up_delta = (hidden_grad * activated).astype(jnp.bfloat16)

    gu_rows = model_width // n_rep
    packed = packed_weight_grads(recv, gate_delta, up_delta, hidden, n_rep)
    reduced = lax.optimization_barrier(
        lax.psum_scatter(packed, "rep", scatter_dimension=0, tiled=True)
    )
    grad_gate, grad_up, grad_down = unpack_weight_grads(reduced, gu_rows, ff_width)

    expert_out = jnp.dot(hidden, down_mat, preferred_element_type=jnp.float32).astype(jnp.bfloat16)
    row_grads = (
        lax.dot_general(gate_delta, gate_mat, contract, preferred_element_type=jnp.float32)
        + lax.dot_general(up_delta, up_mat, contract, preferred_element_type=jnp.float32)
    ).astype(jnp.bfloat16)
    back = jnp.concatenate([expert_out, row_grads], axis=1).reshape(
        n_experts, capacity, 2 * model_width
    )
    returned = lax.all_to_all(back, "ep", split_axis=0, concat_axis=0, tiled=True).reshape(
        slots, 2 * model_width
    )
    pair_back = returned[slot_index]
    pair_out = pair_back[:, :model_width]
    pair_grads = pair_back[:, model_width:]
    layer_out = jnp.sum(
        (weights * pair_out.astype(jnp.float32)).reshape(tok_rows, top_count, model_width), axis=1
    ).astype(jnp.bfloat16)
    gate_grads = jnp.einsum(
        "tkd,td->tk",
        pair_out.reshape(tok_rows, top_count, model_width),
        cotangent,
        preferred_element_type=jnp.float32,
    ).astype(jnp.bfloat16)
    input_grads = jnp.sum(
        pair_grads.astype(jnp.float32).reshape(tok_rows, top_count, model_width), axis=1
    ).astype(jnp.bfloat16)
    return (layer_out, input_grads, gate_grads, grad_gate[None], grad_up[None], grad_down[None])


def solution(mesh):
    in_specs = (
        P(("rep", "ep"), None),
        P(("rep", "ep"), None),
        P(("rep", "ep"), None),
        P("ep", None, None),
        P("ep", None, None),
        P("ep", None, None),
        P(("rep", "ep"), None),
    )
    out_specs = (
        P(("rep", "ep"), None),
        P(("rep", "ep"), None),
        P(("rep", "ep"), None),
        P("ep", "rep", None),
        P("ep", "rep", None),
        P("ep", "rep", None),
    )
    return jax.shard_map(body, mesh=mesh, in_specs=in_specs, out_specs=out_specs, check_vma=False)
```

```python
import jax
import jax.numpy as jnp
from jax import lax
from jax.experimental import pallas as pl
from jax.experimental.pallas import tpu as pltpu
from jax.sharding import PartitionSpec as P


TILE_ROWS = 16
LANES = 128


def _pack_kernel(x_ref, dl_ref, h_ref, og_ref, o_ref, down_ref):
    ff = dl_ref.shape[1] // 2
    width = og_ref.shape[1]
    group, chunk, _ = o_ref.shape
    rows = x_ref.shape[1] // group
    down_rows = down_ref.shape[0] // (group * pl.num_programs(0))
    over = 2 * ff - width
    first = (((0,), (0,)), ((), ()))
    r = pl.program_id(0)

    @pl.when(r == 0)
    def _():
        down_ref[...] = lax.dot_general(
            h_ref[...], og_ref[...], first, preferred_element_type=jnp.float32
        )

    x = x_ref[...]
    gu_all = lax.dot_general(x, dl_ref[...], first, preferred_element_type=jnp.float32)
    col_tiles = over // LANES
    extra = rows * over // width
    for c in range(group):
        g = gu_all[c * rows : (c + 1) * rows, :ff]
        u = gu_all[c * rows : (c + 1) * rows, ff:]
        o_ref[c, :rows, :ff] = g.astype(o_ref.dtype)
        o_ref[c, :rows, ff:] = u[:, : width - ff].astype(o_ref.dtype)
        for i in range(rows // TILE_ROWS):
            for j in range(col_tiles):
                q, p = divmod(i * col_tiles + j, width // LANES)
                src = u[i * TILE_ROWS : (i + 1) * TILE_ROWS, width - ff + j * LANES :][:, :LANES]
                o_ref[
                    c, rows + q * TILE_ROWS : rows + (q + 1) * TILE_ROWS, p * LANES : (p + 1) * LANES
                ] = src.astype(o_ref.dtype)
        start = pl.multiple_of((r * group + c) * down_rows, 8)
        o_ref[c, rows + extra :, :] = down_ref[pl.ds(start, down_rows), :].astype(o_ref.dtype)


GROUP = 4


def packed_weight_grads(recv, deltas, hidden, n_rep):
    slots, ff = hidden.shape
    model_width = recv.shape[1] // 2
    gu_rows = model_width // n_rep
    down_rows = ff // n_rep
    extra = gu_rows * (2 * ff - model_width) // model_width
    chunk = gu_rows + extra + down_rows
    flops = 2 * slots * (model_width * 2 * ff + ff * model_width)
    group = GROUP if n_rep % GROUP == 0 else 1
    return pl.pallas_call(
        _pack_kernel,
        grid=(n_rep // group,),
        in_specs=[
            pl.BlockSpec((slots, group * gu_rows), lambda r: (0, r)),
            pl.BlockSpec((slots, 2 * ff), lambda r: (0, 0)),
            pl.BlockSpec((slots, ff), lambda r: (0, 0)),
            pl.BlockSpec((slots, model_width), lambda r: (0, 1)),
        ],
        out_specs=pl.BlockSpec((group, chunk, model_width), lambda r: (r, 0, 0)),
        out_shape=jax.ShapeDtypeStruct((n_rep, chunk, model_width), jnp.bfloat16),
        scratch_shapes=[pltpu.VMEM((ff, model_width), jnp.float32)],
        compiler_params=pltpu.CompilerParams(dimension_semantics=("arbitrary",)),
        cost_estimate=pl.CostEstimate(
            flops=flops, transcendentals=0, bytes_accessed=2 * n_rep * chunk * model_width
        ),
    )(recv, deltas, hidden, recv)


def _unpack_kernel(red_ref, g_ref, u_ref, d_ref):
    rows, ff = g_ref.shape
    width = red_ref.shape[2]
    over = 2 * ff - width
    extra = rows * over // width
    g_ref[...] = red_ref[0, :rows, :ff].astype(g_ref.dtype)
    u_ref[:, : width - ff] = red_ref[0, :rows, ff:].astype(u_ref.dtype)
    col_tiles = over // LANES
    for i in range(rows // TILE_ROWS):
        for j in range(col_tiles):
            q, p = divmod(i * col_tiles + j, width // LANES)
            col = width - ff + j * LANES
            u_ref[i * TILE_ROWS : (i + 1) * TILE_ROWS, col : col + LANES] = red_ref[
                0, rows + q * TILE_ROWS : rows + (q + 1) * TILE_ROWS, p * LANES : (p + 1) * LANES
            ].astype(u_ref.dtype)
    d_ref[...] = red_ref[0, rows + extra :, :].astype(d_ref.dtype)


def unpack_weight_grads(red, gu_rows, ff):
    _, chunk, width = red.shape
    extra = gu_rows * (2 * ff - width) // width
    return pl.pallas_call(
        _unpack_kernel,
        out_shape=(
            jax.ShapeDtypeStruct((gu_rows, ff), jnp.float32),
            jax.ShapeDtypeStruct((gu_rows, ff), jnp.float32),
            jax.ShapeDtypeStruct((chunk - gu_rows - extra, width), jnp.float32),
        ),
    )(red)


def body(tokens, experts, gates, w_gate, w_up, w_down, cotangent):
    tok_rows, model_width = tokens.shape
    top_count = experts.shape[1]
    n_experts = lax.axis_size("ep")
    n_rep = lax.axis_size("rep")
    capacity = 3 * tok_rows * top_count // (2 * n_experts)
    pair_count = tok_rows * top_count
    gate_mat, up_mat, down_mat = (w_gate[0], w_up[0], w_down[0])
    ff_width = gate_mat.shape[1]
    slots = n_experts * capacity

    flat_exp = experts.reshape(pair_count)
    onehot = (flat_exp[:, None] == jnp.arange(n_experts, dtype=jnp.int32)[None, :]).astype(
        jnp.int32
    )
    slot_rank = jnp.sum((jnp.cumsum(onehot, axis=0) - onehot) * onehot, axis=1)
    slot_index = flat_exp * capacity + slot_rank
    hit = (
        slot_index.reshape(tok_rows, top_count, 1)
        == jnp.arange(slots, dtype=jnp.int32)[None, None, :]
    )
    select = jnp.sum(hit, axis=1).astype(jnp.bfloat16)
    gate_select = jnp.sum(jnp.where(hit, gates[:, :, None], 0), axis=1).astype(jnp.bfloat16)
    rows_first = (((0,), (0,)), ((), ()))
    tok_rows_out = lax.dot_general(select, tokens, rows_first, preferred_element_type=jnp.float32)
    scaled_rows = lax.dot_general(
        gate_select, cotangent, rows_first, preferred_element_type=jnp.float32
    )
    weights = gates.reshape(pair_count, 1).astype(jnp.float32)

    disp = jnp.concatenate(
        [tok_rows_out.astype(jnp.bfloat16), scaled_rows.astype(jnp.bfloat16)], axis=1
    ).reshape(n_experts, capacity, 2 * model_width)
    recv = lax.all_to_all(disp, "ep", split_axis=0, concat_axis=0, tiled=True).reshape(
        slots, 2 * model_width
    )
    rows_in = recv[:, :model_width]
    out_grads = recv[:, model_width:]

    contract = (((1,), (1,)), ((), ()))
    gate_pre = jnp.dot(rows_in, gate_mat, preferred_element_type=jnp.float32)
    up_pre = jnp.dot(rows_in, up_mat, preferred_element_type=jnp.float32)
    sigmoid_g = jax.nn.sigmoid(gate_pre)
    activated = gate_pre * sigmoid_g
    hidden = (activated * up_pre).astype(jnp.bfloat16)
    hidden_grad = lax.dot_general(out_grads, down_mat, contract, preferred_element_type=jnp.float32)
    gate_delta = (hidden_grad * up_pre * sigmoid_g * (1.0 + gate_pre * (1.0 - sigmoid_g))).astype(
        jnp.bfloat16
    )
    up_delta = (hidden_grad * activated).astype(jnp.bfloat16)

    gu_rows = model_width // n_rep
    deltas = jnp.concatenate([gate_delta, up_delta], axis=1)
    packed = packed_weight_grads(recv, deltas, hidden, n_rep)
    reduced = lax.optimization_barrier(
        lax.psum_scatter(packed, "rep", scatter_dimension=0, tiled=True)
    )
    grad_gate, grad_up, grad_down = unpack_weight_grads(reduced, gu_rows, ff_width)

    expert_out = jnp.dot(hidden, down_mat, preferred_element_type=jnp.float32).astype(jnp.bfloat16)
    row_grads = (
        lax.dot_general(gate_delta, gate_mat, contract, preferred_element_type=jnp.float32)
        + lax.dot_general(up_delta, up_mat, contract, preferred_element_type=jnp.float32)
    ).astype(jnp.bfloat16)
    back = jnp.concatenate([expert_out, row_grads], axis=1).reshape(
        n_experts, capacity, 2 * model_width
    )
    returned = lax.all_to_all(back, "ep", split_axis=0, concat_axis=0, tiled=True).reshape(
        slots, 2 * model_width
    )
    pair_back = returned[slot_index]
    pair_out = pair_back[:, :model_width]
    pair_grads = pair_back[:, model_width:]
    layer_out = jnp.sum(
        (weights * pair_out.astype(jnp.float32)).reshape(tok_rows, top_count, model_width), axis=1
    ).astype(jnp.bfloat16)
    gate_grads = jnp.einsum(
        "tkd,td->tk",
        pair_out.reshape(tok_rows, top_count, model_width),
        cotangent,
        preferred_element_type=jnp.float32,
    ).astype(jnp.bfloat16)
    input_grads = jnp.sum(
        pair_grads.astype(jnp.float32).reshape(tok_rows, top_count, model_width), axis=1
    ).astype(jnp.bfloat16)
    return (layer_out, input_grads, gate_grads, grad_gate[None], grad_up[None], grad_down[None])


def solution(mesh):
    in_specs = (
        P(("rep", "ep"), None),
        P(("rep", "ep"), None),
        P(("rep", "ep"), None),
        P("ep", None, None),
        P("ep", None, None),
        P("ep", None, None),
        P(("rep", "ep"), None),
    )
    out_specs = (
        P(("rep", "ep"), None),
        P(("rep", "ep"), None),
        P(("rep", "ep"), None),
        P("ep", "rep", None),
        P("ep", "rep", None),
        P("ep", "rep", None),
    )
    return jax.shard_map(body, mesh=mesh, in_specs=in_specs, out_specs=out_specs, check_vma=False)
```

```python
import jax
import jax.numpy as jnp
from jax import lax
from jax.experimental import pallas as pl
from jax.experimental.pallas import tpu as pltpu
from jax.sharding import PartitionSpec as P


TILE_ROWS = 16
LANES = 128


def _pack_kernel(x_ref, gd_ref, ud_ref, h_ref, og_ref, o_ref, down_ref):
    ff = gd_ref.shape[1]
    width = og_ref.shape[1]
    group, chunk, _ = o_ref.shape
    rows = x_ref.shape[1] // group
    down_rows = down_ref.shape[0] // (group * pl.num_programs(0))
    over = 2 * ff - width
    first = (((0,), (0,)), ((), ()))
    r = pl.program_id(0)

    @pl.when(r == 0)
    def _():
        down_ref[...] = lax.dot_general(
            h_ref[...], og_ref[...], first, preferred_element_type=jnp.float32
        )

    x = x_ref[...]
    g_all = lax.dot_general(x, gd_ref[...], first, preferred_element_type=jnp.float32)
    u_all = lax.dot_general(x, ud_ref[...], first, preferred_element_type=jnp.float32)
    col_tiles = over // LANES
    extra = rows * over // width
    for c in range(group):
        g = g_all[c * rows : (c + 1) * rows]
        u = u_all[c * rows : (c + 1) * rows]
        o_ref[c, :rows, :ff] = g.astype(o_ref.dtype)
        o_ref[c, :rows, ff:] = u[:, : width - ff].astype(o_ref.dtype)
        per_row = width // LANES
        for q in range(extra // TILE_ROWS):
            pieces = []
            for p in range(per_row):
                i, j = divmod(q * per_row + p, col_tiles)
                col = width - ff + j * LANES
                pieces.append(u[i * TILE_ROWS : (i + 1) * TILE_ROWS, col : col + LANES])
            o_ref[c, rows + q * TILE_ROWS : rows + (q + 1) * TILE_ROWS, :] = jnp.concatenate(
                pieces, axis=1
            ).astype(o_ref.dtype)
        start = pl.multiple_of((r * group + c) * down_rows, 8)
        o_ref[c, rows + extra :, :] = down_ref[pl.ds(start, down_rows), :].astype(o_ref.dtype)


GROUP = 4


def packed_weight_grads(recv, gate_delta, up_delta, hidden, n_rep):
    slots, ff = gate_delta.shape
    model_width = recv.shape[1] // 2
    gu_rows = model_width // n_rep
    down_rows = ff // n_rep
    extra = gu_rows * (2 * ff - model_width) // model_width
    chunk = gu_rows + extra + down_rows
    flops = 2 * slots * (model_width * 2 * ff + ff * model_width)
    group = GROUP if n_rep % GROUP == 0 else 1
    return pl.pallas_call(
        _pack_kernel,
        grid=(n_rep // group,),
        in_specs=[
            pl.BlockSpec((slots, group * gu_rows), lambda r: (0, r)),
            pl.BlockSpec((slots, ff), lambda r: (0, 0)),
            pl.BlockSpec((slots, ff), lambda r: (0, 0)),
            pl.BlockSpec((slots, ff), lambda r: (0, 0)),
            pl.BlockSpec((slots, model_width), lambda r: (0, 1)),
        ],
        out_specs=pl.BlockSpec((group, chunk, model_width), lambda r: (r, 0, 0)),
        out_shape=jax.ShapeDtypeStruct((n_rep, chunk, model_width), jnp.bfloat16),
        scratch_shapes=[pltpu.VMEM((ff, model_width), jnp.float32)],
        compiler_params=pltpu.CompilerParams(dimension_semantics=("arbitrary",)),
        cost_estimate=pl.CostEstimate(
            flops=flops, transcendentals=0, bytes_accessed=2 * n_rep * chunk * model_width
        ),
    )(recv, gate_delta, up_delta, hidden, recv)


def _unpack_kernel(red_ref, g_ref, u_ref, d_ref):
    rows, ff = g_ref.shape
    width = red_ref.shape[2]
    over = 2 * ff - width
    extra = rows * over // width
    g_ref[...] = red_ref[0, :rows, :ff].astype(g_ref.dtype)
    u_ref[:, : width - ff] = red_ref[0, :rows, ff:].astype(u_ref.dtype)
    col_tiles = over // LANES
    for i in range(rows // TILE_ROWS):
        for j in range(col_tiles):
            q, p = divmod(i * col_tiles + j, width // LANES)
            col = width - ff + j * LANES
            u_ref[i * TILE_ROWS : (i + 1) * TILE_ROWS, col : col + LANES] = red_ref[
                0, rows + q * TILE_ROWS : rows + (q + 1) * TILE_ROWS, p * LANES : (p + 1) * LANES
            ].astype(u_ref.dtype)
    d_ref[...] = red_ref[0, rows + extra :, :].astype(d_ref.dtype)


def unpack_weight_grads(red, gu_rows, ff):
    _, chunk, width = red.shape
    extra = gu_rows * (2 * ff - width) // width
    return pl.pallas_call(
        _unpack_kernel,
        out_shape=(
            jax.ShapeDtypeStruct((gu_rows, ff), jnp.float32),
            jax.ShapeDtypeStruct((gu_rows, ff), jnp.float32),
            jax.ShapeDtypeStruct((chunk - gu_rows - extra, width), jnp.float32),
        ),
    )(red)


def body(tokens, experts, gates, w_gate, w_up, w_down, cotangent):
    tok_rows, model_width = tokens.shape
    top_count = experts.shape[1]
    n_experts = lax.axis_size("ep")
    n_rep = lax.axis_size("rep")
    capacity = 3 * tok_rows * top_count // (2 * n_experts)
    pair_count = tok_rows * top_count
    gate_mat, up_mat, down_mat = (w_gate[0], w_up[0], w_down[0])
    ff_width = gate_mat.shape[1]
    slots = n_experts * capacity

    flat_exp = experts.reshape(pair_count)
    onehot = (flat_exp[:, None] == jnp.arange(n_experts, dtype=jnp.int32)[None, :]).astype(
        jnp.int32
    )
    slot_rank = jnp.sum((jnp.cumsum(onehot, axis=0) - onehot) * onehot, axis=1)
    slot_index = flat_exp * capacity + slot_rank
    hit = (
        slot_index.reshape(tok_rows, top_count, 1)
        == jnp.arange(slots, dtype=jnp.int32)[None, None, :]
    )
    select = jnp.sum(hit, axis=1).astype(jnp.bfloat16)
    gate_select = jnp.sum(jnp.where(hit, gates[:, :, None], 0), axis=1).astype(jnp.bfloat16)
    rows_first = (((0,), (0,)), ((), ()))
    tok_rows_out = lax.dot_general(select, tokens, rows_first, preferred_element_type=jnp.float32)
    scaled_rows = lax.dot_general(
        gate_select, cotangent, rows_first, preferred_element_type=jnp.float32
    )
    weights = gates.reshape(pair_count, 1).astype(jnp.float32)

    disp = jnp.concatenate(
        [tok_rows_out.astype(jnp.bfloat16), scaled_rows.astype(jnp.bfloat16)], axis=1
    ).reshape(n_experts, capacity, 2 * model_width)
    recv = lax.all_to_all(disp, "ep", split_axis=0, concat_axis=0, tiled=True).reshape(
        slots, 2 * model_width
    )
    rows_in = recv[:, :model_width]
    out_grads = recv[:, model_width:]

    contract = (((1,), (1,)), ((), ()))
    gate_pre = jnp.dot(rows_in, gate_mat, preferred_element_type=jnp.float32)
    up_pre = jnp.dot(rows_in, up_mat, preferred_element_type=jnp.float32)
    sigmoid_g = jax.nn.sigmoid(gate_pre)
    activated = gate_pre * sigmoid_g
    hidden = (activated * up_pre).astype(jnp.bfloat16)
    hidden_grad = lax.dot_general(out_grads, down_mat, contract, preferred_element_type=jnp.float32)
    gate_delta = (hidden_grad * up_pre * sigmoid_g * (1.0 + gate_pre * (1.0 - sigmoid_g))).astype(
        jnp.bfloat16
    )
    up_delta = (hidden_grad * activated).astype(jnp.bfloat16)

    gu_rows = model_width // n_rep
    packed = packed_weight_grads(recv, gate_delta, up_delta, hidden, n_rep)
    reduced = lax.optimization_barrier(
        lax.psum_scatter(packed, "rep", scatter_dimension=0, tiled=True)
    )
    grad_gate, grad_up, grad_down = unpack_weight_grads(reduced, gu_rows, ff_width)

    expert_out = jnp.dot(hidden, down_mat, preferred_element_type=jnp.float32).astype(jnp.bfloat16)
    row_grads = (
        lax.dot_general(gate_delta, gate_mat, contract, preferred_element_type=jnp.float32)
        + lax.dot_general(up_delta, up_mat, contract, preferred_element_type=jnp.float32)
    ).astype(jnp.bfloat16)
    back = jnp.concatenate([expert_out, row_grads], axis=1).reshape(
        n_experts, capacity, 2 * model_width
    )
    returned = lax.all_to_all(back, "ep", split_axis=0, concat_axis=0, tiled=True).reshape(
        slots, 2 * model_width
    )
    pair_back = returned[slot_index]
    pair_out = pair_back[:, :model_width]
    pair_grads = pair_back[:, model_width:]
    layer_out = jnp.sum(
        (weights * pair_out.astype(jnp.float32)).reshape(tok_rows, top_count, model_width), axis=1
    ).astype(jnp.bfloat16)
    gate_grads = jnp.einsum(
        "tkd,td->tk",
        pair_out.reshape(tok_rows, top_count, model_width),
        cotangent,
        preferred_element_type=jnp.float32,
    ).astype(jnp.bfloat16)
    input_grads = jnp.sum(
        pair_grads.astype(jnp.float32).reshape(tok_rows, top_count, model_width), axis=1
    ).astype(jnp.bfloat16)
    return (layer_out, input_grads, gate_grads, grad_gate[None], grad_up[None], grad_down[None])


def solution(mesh):
    in_specs = (
        P(("rep", "ep"), None),
        P(("rep", "ep"), None),
        P(("rep", "ep"), None),
        P("ep", None, None),
        P("ep", None, None),
        P("ep", None, None),
        P(("rep", "ep"), None),
    )
    out_specs = (
        P(("rep", "ep"), None),
        P(("rep", "ep"), None),
        P(("rep", "ep"), None),
        P("ep", "rep", None),
        P("ep", "rep", None),
        P("ep", "rep", None),
    )
    return jax.shard_map(body, mesh=mesh, in_specs=in_specs, out_specs=out_specs, check_vma=False)
```

```python
import jax
import jax.numpy as jnp
from jax import lax
from jax.experimental import pallas as pl
from jax.experimental.pallas import tpu as pltpu
from jax.sharding import PartitionSpec as P


TILE_ROWS = 16
LANES = 128


def _pack_kernel(x_ref, gd_ref, ud_ref, h_ref, og_ref, o_ref, down_ref):
    ff = gd_ref.shape[1]
    width = og_ref.shape[1]
    group, chunk, _ = o_ref.shape
    rows = x_ref.shape[1] // group
    down_rows = down_ref.shape[0] // (group * pl.num_programs(0))
    over = 2 * ff - width
    first = (((0,), (0,)), ((), ()))
    r = pl.program_id(0)

    @pl.when(r == 0)
    def _():
        down_ref[...] = lax.dot_general(
            h_ref[...], og_ref[...], first, preferred_element_type=jnp.float32
        )

    x = x_ref[...]
    g_all = lax.dot_general(x, gd_ref[...], first, preferred_element_type=jnp.float32)
    u_all = lax.dot_general(x, ud_ref[...], first, preferred_element_type=jnp.float32)
    col_tiles = over // LANES
    extra = rows * over // width
    for c in range(group):
        g = g_all[c * rows : (c + 1) * rows]
        u = u_all[c * rows : (c + 1) * rows]
        o_ref[c, :rows, :ff] = g.astype(o_ref.dtype)
        o_ref[c, :rows, ff:] = u[:, : width - ff].astype(o_ref.dtype)
        for i in range(rows // TILE_ROWS):
            for j in range(col_tiles):
                q, p = divmod(i * col_tiles + j, width // LANES)
                src = u[i * TILE_ROWS : (i + 1) * TILE_ROWS, width - ff + j * LANES :][:, :LANES]
                o_ref[
                    c, rows + q * TILE_ROWS : rows + (q + 1) * TILE_ROWS, p * LANES : (p + 1) * LANES
                ] = src.astype(o_ref.dtype)
        start = pl.multiple_of((r * group + c) * down_rows, 8)
        o_ref[c, rows + extra :, :] = down_ref[pl.ds(start, down_rows), :].astype(o_ref.dtype)


GROUP = 2


def packed_weight_grads(recv, gate_delta, up_delta, hidden, n_rep):
    slots, ff = gate_delta.shape
    model_width = recv.shape[1] // 2
    gu_rows = model_width // n_rep
    down_rows = ff // n_rep
    extra = gu_rows * (2 * ff - model_width) // model_width
    chunk = gu_rows + extra + down_rows
    flops = 2 * slots * (model_width * 2 * ff + ff * model_width)
    group = GROUP if n_rep % GROUP == 0 else 1
    return pl.pallas_call(
        _pack_kernel,
        grid=(n_rep // group,),
        in_specs=[
            pl.BlockSpec((slots, group * gu_rows), lambda r: (0, r)),
            pl.BlockSpec((slots, ff), lambda r: (0, 0)),
            pl.BlockSpec((slots, ff), lambda r: (0, 0)),
            pl.BlockSpec((slots, ff), lambda r: (0, 0)),
            pl.BlockSpec((slots, model_width), lambda r: (0, 1)),
        ],
        out_specs=pl.BlockSpec((group, chunk, model_width), lambda r: (r, 0, 0)),
        out_shape=jax.ShapeDtypeStruct((n_rep, chunk, model_width), jnp.bfloat16),
        scratch_shapes=[pltpu.VMEM((ff, model_width), jnp.float32)],
        compiler_params=pltpu.CompilerParams(dimension_semantics=("arbitrary",)),
        cost_estimate=pl.CostEstimate(
            flops=flops, transcendentals=0, bytes_accessed=2 * n_rep * chunk * model_width
        ),
    )(recv, gate_delta, up_delta, hidden, recv)


def _unpack_kernel(red_ref, g_ref, u_ref, d_ref):
    rows, ff = g_ref.shape
    width = red_ref.shape[2]
    over = 2 * ff - width
    extra = rows * over // width
    g_ref[...] = red_ref[0, :rows, :ff].astype(g_ref.dtype)
    u_ref[:, : width - ff] = red_ref[0, :rows, ff:].astype(u_ref.dtype)
    col_tiles = over // LANES
    for i in range(rows // TILE_ROWS):
        for j in range(col_tiles):
            q, p = divmod(i * col_tiles + j, width // LANES)
            col = width - ff + j * LANES
            u_ref[i * TILE_ROWS : (i + 1) * TILE_ROWS, col : col + LANES] = red_ref[
                0, rows + q * TILE_ROWS : rows + (q + 1) * TILE_ROWS, p * LANES : (p + 1) * LANES
            ].astype(u_ref.dtype)
    d_ref[...] = red_ref[0, rows + extra :, :].astype(d_ref.dtype)


def unpack_weight_grads(red, gu_rows, ff):
    _, chunk, width = red.shape
    extra = gu_rows * (2 * ff - width) // width
    return pl.pallas_call(
        _unpack_kernel,
        out_shape=(
            jax.ShapeDtypeStruct((gu_rows, ff), jnp.float32),
            jax.ShapeDtypeStruct((gu_rows, ff), jnp.float32),
            jax.ShapeDtypeStruct((chunk - gu_rows - extra, width), jnp.float32),
        ),
    )(red)


def body(tokens, experts, gates, w_gate, w_up, w_down, cotangent):
    tok_rows, model_width = tokens.shape
    top_count = experts.shape[1]
    n_experts = lax.axis_size("ep")
    n_rep = lax.axis_size("rep")
    capacity = 3 * tok_rows * top_count // (2 * n_experts)
    pair_count = tok_rows * top_count
    gate_mat, up_mat, down_mat = (w_gate[0], w_up[0], w_down[0])
    ff_width = gate_mat.shape[1]
    slots = n_experts * capacity

    flat_exp = experts.reshape(pair_count)
    onehot = (flat_exp[:, None] == jnp.arange(n_experts, dtype=jnp.int32)[None, :]).astype(
        jnp.int32
    )
    slot_rank = jnp.sum((jnp.cumsum(onehot, axis=0) - onehot) * onehot, axis=1)
    slot_index = flat_exp * capacity + slot_rank
    hit = (
        slot_index.reshape(tok_rows, top_count, 1)
        == jnp.arange(slots, dtype=jnp.int32)[None, None, :]
    )
    select = jnp.sum(hit, axis=1).astype(jnp.bfloat16)
    gate_select = jnp.sum(jnp.where(hit, gates[:, :, None], 0), axis=1).astype(jnp.bfloat16)
    rows_first = (((0,), (0,)), ((), ()))
    tok_rows_out = lax.dot_general(select, tokens, rows_first, preferred_element_type=jnp.float32)
    scaled_rows = lax.dot_general(
        gate_select, cotangent, rows_first, preferred_element_type=jnp.float32
    )
    weights = gates.reshape(pair_count, 1).astype(jnp.float32)

    disp = jnp.concatenate(
        [tok_rows_out.astype(jnp.bfloat16), scaled_rows.astype(jnp.bfloat16)], axis=1
    ).reshape(n_experts, capacity, 2 * model_width)
    recv = lax.all_to_all(disp, "ep", split_axis=0, concat_axis=0, tiled=True).reshape(
        slots, 2 * model_width
    )
    rows_in = recv[:, :model_width]
    out_grads = recv[:, model_width:]

    contract = (((1,), (1,)), ((), ()))
    gate_pre = jnp.dot(rows_in, gate_mat, preferred_element_type=jnp.float32)
    up_pre = jnp.dot(rows_in, up_mat, preferred_element_type=jnp.float32)
    sigmoid_g = jax.nn.sigmoid(gate_pre)
    activated = gate_pre * sigmoid_g
    hidden = (activated * up_pre).astype(jnp.bfloat16)
    hidden_grad = lax.dot_general(out_grads, down_mat, contract, preferred_element_type=jnp.float32)
    gate_delta = (hidden_grad * up_pre * sigmoid_g * (1.0 + gate_pre * (1.0 - sigmoid_g))).astype(
        jnp.bfloat16
    )
    up_delta = (hidden_grad * activated).astype(jnp.bfloat16)

    gu_rows = model_width // n_rep
    packed = packed_weight_grads(recv, gate_delta, up_delta, hidden, n_rep)
    reduced = lax.optimization_barrier(
        lax.psum_scatter(packed, "rep", scatter_dimension=0, tiled=True)
    )
    grad_gate, grad_up, grad_down = unpack_weight_grads(reduced, gu_rows, ff_width)

    expert_out = jnp.dot(hidden, down_mat, preferred_element_type=jnp.float32).astype(jnp.bfloat16)
    row_grads = (
        lax.dot_general(gate_delta, gate_mat, contract, preferred_element_type=jnp.float32)
        + lax.dot_general(up_delta, up_mat, contract, preferred_element_type=jnp.float32)
    ).astype(jnp.bfloat16)
    back = jnp.concatenate([expert_out, row_grads], axis=1).reshape(
        n_experts, capacity, 2 * model_width
    )
    returned = lax.all_to_all(back, "ep", split_axis=0, concat_axis=0, tiled=True).reshape(
        slots, 2 * model_width
    )
    pair_back = returned[slot_index]
    pair_out = pair_back[:, :model_width]
    pair_grads = pair_back[:, model_width:]
    layer_out = jnp.sum(
        (weights * pair_out.astype(jnp.float32)).reshape(tok_rows, top_count, model_width), axis=1
    ).astype(jnp.bfloat16)
    gate_grads = jnp.einsum(
        "tkd,td->tk",
        pair_out.reshape(tok_rows, top_count, model_width),
        cotangent,
        preferred_element_type=jnp.float32,
    ).astype(jnp.bfloat16)
    input_grads = jnp.sum(
        pair_grads.astype(jnp.float32).reshape(tok_rows, top_count, model_width), axis=1
    ).astype(jnp.bfloat16)
    return (layer_out, input_grads, gate_grads, grad_gate[None], grad_up[None], grad_down[None])


def solution(mesh):
    in_specs = (
        P(("rep", "ep"), None),
        P(("rep", "ep"), None),
        P(("rep", "ep"), None),
        P("ep", None, None),
        P("ep", None, None),
        P("ep", None, None),
        P(("rep", "ep"), None),
    )
    out_specs = (
        P(("rep", "ep"), None),
        P(("rep", "ep"), None),
        P(("rep", "ep"), None),
        P("ep", "rep", None),
        P("ep", "rep", None),
        P("ep", "rep", None),
    )
    return jax.shard_map(body, mesh=mesh, in_specs=in_specs, out_specs=out_specs, check_vma=False)
```
